256 devices in a mesh: depth: 16 (over y, z_hi), chan: 16 (over x, z_lo, core).
Axes of the slice: x: 4, y: 4, z: 8 (z_hi: 4, z_lo: 2; z = z_hi * 2 + z_lo), core: 2. Of those that a mesh axis runs over, the one named last changes fastest.
Arguments:
- volume: bfloat16 [256, 16, 4096], P('chan', 'depth'), may hold values from -6 to 6
- w_first: bfloat16 [27, 256, 256], P(None, 'chan'), may hold values from -0.078125 to 0.078125
- b_first: float32 [256], P('chan'), may hold values from -3 to 3
- w_second: bfloat16 [27, 256, 256], P(None, None, 'chan'), may hold values from -0.078125 to 0.078125
- b_second: float32 [256], P('chan'), may hold values from -3 to 3
Outputs:
- block_out: bfloat16 [256, 16, 4096], P('chan', 'depth')
The draws below stay inside these ranges and needn't reach their ends.
All inputs are finite; a program needn't handle non-finite values.
Results may differ from the reference program's by a relative error of at most 0.0043.
Values may be sent and summed in bfloat16 or wider, within the bound.
No kernel may reach another device: no remote copies, remote signals or barrier semaphores. Data moves between devices by JAX's collectives and lax.ppermute only.
A program may use at most 128 MiB of HBM per device.

```python
import jax
import jax.numpy as jnp
from jax import lax

C = 256
H = 64
W = 64
D = 16
HW = 4096


def level_of(key, extent, pieces, low, top_value):
    loudness = 1.0
    for position, parts in pieces:
        draws = jax.random.uniform(jax.random.fold_in(jax.random.fold_in(key, 6), position), (parts,), jnp.float32, low / len(pieces), top_value / len(pieces))
        loudness = loudness * jnp.repeat(jnp.exp(draws), extent[position] // parts).reshape((-1,) + (1,) * (len(extent) - 1 - position))
    return loudness


def normal_values(own_key, shape, width, limit, cuts=(), held_as=jnp.bfloat16):
    level = level_of(own_key, shape, cuts, -0.22, 0.18) if cuts else 1.0
    entries = jax.random.normal(own_key, shape, jnp.float32) * width * level
    return jnp.minimum(jnp.maximum(entries, -limit), limit).astype(held_as)


def setup_inputs(seed: int = 0) -> dict:
    arg_keys = jax.random.split(jax.random.key(seed), 6)
    volume = normal_values(arg_keys[0], (C, D, HW), 1.0, 6.0, ((0, 16), (1, 16)))
    w_first = normal_values(arg_keys[1], (27, C, C), (27 * C) ** -0.5, 0.078125, ((1, 16),))
    b_first = normal_values(arg_keys[2], (C,), 0.5, 3.0, ((0, 16),), jnp.float32)
    w_second = normal_values(arg_keys[3], (27, C, C), (27 * C) ** -0.5, 0.078125, ((2, 16),))
    b_second = normal_values(arg_keys[4], (C,), 0.5, 3.0, ((0, 16),), jnp.float32)
    return {"volume": volume, "w_first": w_first, "b_first": b_first, "w_second": w_second, "b_second": b_second}


def convolve(source, filters):
    in_chan, planes, cell_count = source.shape
    out_chan = filters.shape[2]
    volume_f = source.astype(jnp.float32).reshape(1, in_chan, planes, H, W)
    kernel = filters.astype(jnp.float32).reshape(3, 3, 3, in_chan, out_chan).transpose(4, 3, 0, 1, 2)
    result = lax.conv_general_dilated(volume_f, kernel, (1, 1, 1), ((1, 1), (1, 1), (1, 1)),
                                      dimension_numbers=("NCDHW", "OIDHW", "NCDHW"),
                                      precision=lax.Precision.HIGHEST)
    return result.reshape(out_chan, planes, cell_count)


def reference(volume, w_first, b_first, w_second, b_second):
    first_sum = convolve(volume, w_first) + b_first[:, None, None]
    hidden = jnp.maximum(first_sum, 0.0).astype(jnp.bfloat16)
    second_sum = convolve(hidden, w_second) + b_second[:, None, None]
    return second_sum.astype(jnp.bfloat16)
```

```python
import jax
import jax.numpy as jnp
from jax import lax
from jax.experimental import pallas as pl
from jax.experimental.pallas import tpu as pltpu
from jax.sharding import PartitionSpec as P

W = 64


def plane_kernel(w_ref, x_ref, o_ref):
    out_chan = o_ref.shape[1]
    cell_count = x_ref.shape[1]
    x = x_ref[...]
    cell = lax.broadcasted_iota(jnp.int32, (out_chan, cell_count), 1)
    row = lax.shift_right_logical(cell, W.bit_length() - 1)
    col = cell & (W - 1)
    rows = cell_count // W
    masks = []
    for kh in range(3):
        for kw in range(3):
            ok = None
            if kh == 0:
                ok = row >= 1
            elif kh == 2:
                ok = row < rows - 1
            if kw == 0:
                ok = (col >= 1) if ok is None else ok & (col >= 1)
            elif kw == 2:
                ok = (col < W - 1) if ok is None else ok & (col < W - 1)
            masks.append(ok)
    for kd in range(3):
        z = jnp.dot(w_ref[kd], x, preferred_element_type=jnp.float32)
        acc = None
        for kh in range(3):
            for kw in range(3):
                t = kh * 3 + kw
                shift = (kh - 1) * W + (kw - 1)
                zt = z[t * out_chan : (t + 1) * out_chan]
                if shift != 0:
                    zt = pltpu.roll(zt, (-shift) % cell_count, 1)
                if masks[t] is not None:
                    zt = jnp.where(masks[t], zt, 0.0)
                acc = zt if acc is None else acc + zt
        o_ref[kd] = acc


def plane_partials(wk, x):
    out_chan = wk.shape[1] // 9
    cell_count = x.shape[1]
    return pl.pallas_call(
        plane_kernel,
        out_shape=jax.ShapeDtypeStruct((3, out_chan, cell_count), jnp.float32),
        compiler_params=pltpu.CompilerParams(vmem_limit_bytes=48 * 1024 * 1024),
    )(wk, x)


def kernel_filters(filters):
    taps, in_chan, out_chan = filters.shape
    f = filters.reshape(3, 9, in_chan, out_chan).transpose(0, 1, 3, 2)
    return f.reshape(3, 9 * out_chan, in_chan)


def depth_combine(partials):
    peers = lax.axis_size("depth")
    up = [(i, i + 1) for i in range(peers - 1)]
    down = [(j, i) for i, j in up]
    from_below = lax.ppermute(partials[-1, 0], "depth", up)
    from_above = lax.ppermute(partials[0, 2], "depth", down)
    planes = partials.shape[0]
    lower = [from_below] + [partials[p - 1, 0] for p in range(1, planes)]
    upper = [partials[p + 1, 2] for p in range(planes - 1)] + [from_above]
    return jnp.stack([partials[p, 1] + lower[p] + upper[p] for p in range(planes)], 0)


def layer(wk, source):
    planes = source.shape[1]
    partials = jnp.stack([plane_partials(wk, source[:, p]) for p in range(planes)], 0)
    return depth_combine(partials)


def body(volume, w_first, b_first, w_second, b_second):
    chan_local, slab_depth, cell_count = volume.shape
    w1 = lax.all_to_all(w_first, "chan", 2, 1, tiled=True)
    w1k = kernel_filters(w1)
    w2k = kernel_filters(w_second)
    full_volume = lax.all_gather(volume, "chan", axis=0, tiled=True)
    first_sum = layer(w1k, full_volume)
    hidden = jnp.maximum(first_sum + b_first[None, :, None], 0.0).astype(jnp.bfloat16)
    hidden = hidden.transpose(1, 0, 2)
    full_hidden = lax.all_gather(hidden, "chan", axis=0, tiled=True)
    second_sum = layer(w2k, full_hidden)
    block_out = (second_sum + b_second[None, :, None]).astype(jnp.bfloat16)
    return block_out.transpose(1, 0, 2)


def solution(mesh):
    in_specs = (
        P("chan", "depth", None),
        P(None, "chan", None),
        P("chan"),
        P(None, None, "chan"),
        P("chan"),
    )
    out_specs = P("chan", "depth", None)
    return jax.shard_map(body, mesh=mesh, in_specs=in_specs, out_specs=out_specs, check_vma=False)
```

```python
import jax
import jax.numpy as jnp
from jax import lax
from jax.experimental import pallas as pl
from jax.experimental.pallas import tpu as pltpu
from jax.sharding import PartitionSpec as P

W = 64


def plane_kernel(w_ref, x_ref, o_ref):
    out_chan = o_ref.shape[1]
    cell_count = x_ref.shape[1]
    x = x_ref[...]
    cell = lax.broadcasted_iota(jnp.int32, (out_chan, cell_count), 1)
    row = lax.shift_right_logical(cell, W.bit_length() - 1)
    col = cell & (W - 1)
    rows = cell_count // W
    masks = []
    for kh in range(3):
        for kw in range(3):
            ok = None
            if kh == 0:
                ok = row >= 1
            elif kh == 2:
                ok = row < rows - 1
            if kw == 0:
                ok = (col >= 1) if ok is None else ok & (col >= 1)
            elif kw == 2:
                ok = (col < W - 1) if ok is None else ok & (col < W - 1)
            masks.append(ok)
    for kd in range(3):
        z = jnp.dot(w_ref[kd], x, preferred_element_type=jnp.float32)
        acc = None
        for kh in range(3):
            for kw in range(3):
                t = kh * 3 + kw
                shift = (kh - 1) * W + (kw - 1)
                zt = z[t * out_chan : (t + 1) * out_chan]
                if shift != 0:
                    zt = pltpu.roll(zt, (-shift) % cell_count, 1)
                if masks[t] is not None:
                    zt = jnp.where(masks[t], zt, 0.0)
                acc = zt if acc is None else acc + zt
        o_ref[kd] = acc


def plane_partials(wk, x):
    out_chan = wk.shape[1] // 9
    cell_count = x.shape[1]
    return pl.pallas_call(
        plane_kernel,
        out_shape=jax.ShapeDtypeStruct((3, out_chan, cell_count), jnp.float32),
        compiler_params=pltpu.CompilerParams(vmem_limit_bytes=48 * 1024 * 1024),
    )(wk, x)


def kernel_filters(filters):
    taps, in_chan, out_chan = filters.shape
    f = filters.reshape(3, 9, in_chan, out_chan).transpose(0, 1, 3, 2)
    return f.reshape(3, 9 * out_chan, in_chan)


def depth_combine(partials):
    peers = lax.axis_size("depth")
    up = [(i, i + 1) for i in range(peers - 1)]
    down = [(j, i) for i, j in up]
    from_below = lax.ppermute(partials[-1, 0], "depth", up)
    from_above = lax.ppermute(partials[0, 2], "depth", down)
    planes = partials.shape[0]
    lower = [from_below] + [partials[p - 1, 0] for p in range(1, planes)]
    upper = [partials[p + 1, 2] for p in range(planes - 1)] + [from_above]
    return jnp.stack([partials[p, 1] + lower[p] + upper[p] for p in range(planes)], 0)


def layer(wk, source):
    planes = source.shape[1]
    partials = jnp.stack([plane_partials(wk, source[:, p]) for p in range(planes)], 0)
    return depth_combine(partials)


def gather_chan(local, extra=None):
    peers = lax.axis_size("chan")
    flat = local.reshape(1, -1)
    sent = jnp.broadcast_to(flat, (peers, flat.shape[1]))
    if extra is not None:
        sent = jnp.concatenate([sent, extra.astype(sent.dtype)], 1)
    got = lax.all_to_all(sent, "chan", 0, 0, tiled=True)
    full = got[:, : flat.shape[1]].reshape((peers * local.shape[0],) + local.shape[1:])
    return full, got[:, flat.shape[1] :]


def body(volume, w_first, b_first, w_second, b_second):
    chan_local, slab_depth, cell_count = volume.shape
    peers = lax.axis_size("chan")
    taps, in_local, out_chan = w_first.shape
    out_local = out_chan // peers
    w_parts = w_first.reshape(3, 9, in_local, peers, out_local).transpose(3, 0, 1, 4, 2)
    full_volume, w_got = gather_chan(volume, w_parts.reshape(peers, -1))
    w1k = (
        w_got.reshape(peers, 3, 9, out_local, in_local)
        .transpose(1, 2, 3, 0, 4)
        .reshape(3, 9 * out_local, peers * in_local)
    )
    w2k = kernel_filters(w_second)
    first_sum = layer(w1k, full_volume)
    hidden = jnp.maximum(first_sum + b_first[None, :, None], 0.0).astype(jnp.bfloat16)
    hidden = hidden.transpose(1, 0, 2)
    full_hidden, _ = gather_chan(hidden)
    second_sum = layer(w2k, full_hidden)
    block_out = (second_sum + b_second[None, :, None]).astype(jnp.bfloat16)
    return block_out.transpose(1, 0, 2)


def solution(mesh):
    in_specs = (
        P("chan", "depth", None),
        P(None, "chan", None),
        P("chan"),
        P(None, None, "chan"),
        P("chan"),
    )
    out_specs = P("chan", "depth", None)
    return jax.shard_map(body, mesh=mesh, in_specs=in_specs, out_specs=out_specs, check_vma=False)
```

```python
import jax
import jax.numpy as jnp
from jax import lax
from jax.experimental import pallas as pl
from jax.experimental.pallas import tpu as pltpu
from jax.sharding import PartitionSpec as P

W = 64


def plane_kernel(w_ref, x_ref, o_ref):
    out_chan = o_ref.shape[1]
    cell_count = x_ref.shape[1]
    x = x_ref[...]
    cell = lax.broadcasted_iota(jnp.int32, (out_chan, cell_count), 1)
    row = lax.shift_right_logical(cell, W.bit_length() - 1)
    col = cell & (W - 1)
    rows = cell_count // W
    masks = []
    for kh in range(3):
        for kw in range(3):
            ok = None
            if kh == 0:
                ok = row >= 1
            elif kh == 2:
                ok = row < rows - 1
            if kw == 0:
                ok = (col >= 1) if ok is None else ok & (col >= 1)
            elif kw == 2:
                ok = (col < W - 1) if ok is None else ok & (col < W - 1)
            masks.append(ok)
    for kd in range(3):
        z = jnp.dot(w_ref[kd], x, preferred_element_type=jnp.float32)
        acc = None
        for kh in range(3):
            for kw in range(3):
                t = kh * 3 + kw
                shift = (kh - 1) * W + (kw - 1)
                zt = z[t * out_chan : (t + 1) * out_chan]
                if shift != 0:
                    zt = pltpu.roll(zt, (-shift) % cell_count, 1)
                if masks[t] is not None:
                    zt = jnp.where(masks[t], zt, 0.0)
                acc = zt if acc is None else acc + zt
        o_ref[kd] = acc


def plane_partials(wk, x):
    out_chan = wk.shape[1] // 9
    cell_count = x.shape[1]
    return pl.pallas_call(
        plane_kernel,
        out_shape=jax.ShapeDtypeStruct((3, out_chan, cell_count), jnp.float32),
        compiler_params=pltpu.CompilerParams(vmem_limit_bytes=48 * 1024 * 1024),
    )(wk, x)


def kernel_filters(filters):
    taps, in_chan, out_chan = filters.shape
    f = filters.reshape(3, 9, in_chan, out_chan).transpose(0, 1, 3, 2)
    return f.reshape(3, 9 * out_chan, in_chan)


def depth_combine(partials):
    peers = lax.axis_size("depth")
    up = [(i, i + 1) for i in range(peers - 1)]
    down = [(j, i) for i, j in up]
    from_below = lax.ppermute(partials[-1, 0], "depth", up)
    from_above = lax.ppermute(partials[0, 2], "depth", down)
    planes = partials.shape[0]
    lower = [from_below] + [partials[p - 1, 0] for p in range(1, planes)]
    upper = [partials[p + 1, 2] for p in range(planes - 1)] + [from_above]
    return jnp.stack([partials[p, 1] + lower[p] + upper[p] for p in range(planes)], 0)


def layer(wk, source):
    planes = source.shape[1]
    partials = jnp.stack([plane_partials(wk, source[:, p]) for p in range(planes)], 0)
    return depth_combine(partials)


CHAN = ("chip", "core")


def gather_chan(local):
    pair = lax.all_gather(local, "core", axis=0, tiled=True)
    return lax.all_gather(pair, "chip", axis=0, tiled=True)


def body(volume, w_first, b_first, w_second, b_second):
    chan_local, slab_depth, cell_count = volume.shape
    w1 = lax.all_to_all(w_first, CHAN, 2, 1, tiled=True)
    w1k = kernel_filters(w1)
    w2k = kernel_filters(w_second)
    full_volume = gather_chan(volume)
    first_sum = layer(w1k, full_volume)
    hidden = jnp.maximum(first_sum + b_first[None, :, None], 0.0).astype(jnp.bfloat16)
    hidden = hidden.transpose(1, 0, 2)
    full_hidden = gather_chan(hidden)
    second_sum = layer(w2k, full_hidden)
    block_out = (second_sum + b_second[None, :, None]).astype(jnp.bfloat16)
    return block_out.transpose(1, 0, 2)


def solution(mesh):
    depth, chan = mesh.devices.shape
    split = jax.sharding.Mesh(mesh.devices.reshape(depth, chan // 2, 2), ("depth",) + CHAN)
    in_specs = (
        P(CHAN, "depth", None),
        P(None, CHAN, None),
        P(CHAN),
        P(None, None, CHAN),
        P(CHAN),
    )
    out_specs = P(CHAN, "depth", None)
    return jax.shard_map(body, mesh=split, in_specs=in_specs, out_specs=out_specs, check_vma=False)
```

```python
import jax
import jax.numpy as jnp
from jax import lax
from jax.experimental import pallas as pl
from jax.experimental.pallas import tpu as pltpu
from jax.sharding import PartitionSpec as P

W = 64


def plane_kernel(w_ref, x_ref, o_ref):
    out_chan = o_ref.shape[1]
    cell_count = x_ref.shape[1]
    x = x_ref[...]
    cell = lax.broadcasted_iota(jnp.int32, (out_chan, cell_count), 1)
    row = lax.shift_right_logical(cell, W.bit_length() - 1)
    col = cell & (W - 1)
    rows = cell_count // W
    masks = []
    for kh in range(3):
        for kw in range(3):
            ok = None
            if kh == 0:
                ok = row >= 1
            elif kh == 2:
                ok = row < rows - 1
            if kw == 0:
                ok = (col >= 1) if ok is None else ok & (col >= 1)
            elif kw == 2:
                ok = (col < W - 1) if ok is None else ok & (col < W - 1)
            masks.append(ok)
    for kd in range(3):
        z = jnp.dot(w_ref[kd], x, preferred_element_type=jnp.float32)
        acc = None
        for kh in range(3):
            for kw in range(3):
                t = kh * 3 + kw
                shift = (kh - 1) * W + (kw - 1)
                zt = z[t * out_chan : (t + 1) * out_chan]
                if shift != 0:
                    zt = pltpu.roll(zt, (-shift) % cell_count, 1)
                if masks[t] is not None:
                    zt = jnp.where(masks[t], zt, 0.0)
                acc = zt if acc is None else acc + zt
        o_ref[kd] = acc


def plane_partials(wk, x):
    out_chan = wk.shape[1] // 9
    cell_count = x.shape[1]
    return pl.pallas_call(
        plane_kernel,
        out_shape=jax.ShapeDtypeStruct((3, out_chan, cell_count), jnp.float32),
        compiler_params=pltpu.CompilerParams(vmem_limit_bytes=48 * 1024 * 1024),
    )(wk, x)


def kernel_filters(filters):
    taps, in_chan, out_chan = filters.shape
    f = filters.reshape(3, 9, in_chan, out_chan).transpose(0, 1, 3, 2)
    return f.reshape(3, 9 * out_chan, in_chan)


def depth_combine(partials):
    peers = lax.axis_size("depth")
    up = [(i, i + 1) for i in range(peers - 1)]
    down = [(j, i) for i, j in up]
    from_below = lax.ppermute(partials[-1, 0], "depth", up)
    from_above = lax.ppermute(partials[0, 2], "depth", down)
    planes = partials.shape[0]
    lower = [from_below] + [partials[p - 1, 0] for p in range(1, planes)]
    upper = [partials[p + 1, 2] for p in range(planes - 1)] + [from_above]
    return jnp.stack([partials[p, 1] + lower[p] + upper[p] for p in range(planes)], 0)


def layer(wk, source):
    planes = source.shape[1]
    partials = jnp.stack([plane_partials(wk, source[:, p]) for p in range(planes)], 0)
    return depth_combine(partials)


CHAN = ("chip", "core")


def gather_chan(local):
    pair = lax.all_gather(local, "core", axis=0, tiled=True)
    n = lax.axis_size("chip")
    got = [pair] + [
        lax.ppermute(pair, "chip", [(i, (i + k) % n) for i in range(n)]) for k in range(1, n)
    ]
    return jnp.concatenate(got, 0)


def match_order(wk):
    n = lax.axis_size("chip")
    me = lax.axis_index("chip")
    order = (me - jnp.arange(n)) % n
    taps, rows, in_chan = wk.shape
    blocks = jnp.take(wk.reshape(taps, rows, n, in_chan // n), order, axis=2)
    return blocks.reshape(taps, rows, in_chan)


def body(volume, w_first, b_first, w_second, b_second):
    chan_local, slab_depth, cell_count = volume.shape
    w1 = lax.all_to_all(w_first, CHAN, 2, 1, tiled=True)
    w1k = match_order(kernel_filters(w1))
    w2k = match_order(kernel_filters(w_second))
    full_volume = gather_chan(volume)
    first_sum = layer(w1k, full_volume)
    hidden = jnp.maximum(first_sum + b_first[None, :, None], 0.0).astype(jnp.bfloat16)
    hidden = hidden.transpose(1, 0, 2)
    full_hidden = gather_chan(hidden)
    second_sum = layer(w2k, full_hidden)
    block_out = (second_sum + b_second[None, :, None]).astype(jnp.bfloat16)
    return block_out.transpose(1, 0, 2)


def solution(mesh):
    depth, chan = mesh.devices.shape
    split = jax.sharding.Mesh(mesh.devices.reshape(depth, chan // 2, 2), ("depth",) + CHAN)
    in_specs = (
        P(CHAN, "depth", None),
        P(None, CHAN, None),
        P(CHAN),
        P(None, None, CHAN),
        P(CHAN),
    )
    out_specs = P(CHAN, "depth", None)
    return jax.shard_map(body, mesh=split, in_specs=in_specs, out_specs=out_specs, check_vma=False)
```

```python
import jax
import jax.numpy as jnp
from jax import lax
from jax.experimental import pallas as pl
from jax.experimental.pallas import tpu as pltpu
from jax.sharding import PartitionSpec as P

W = 64


def plane_kernel(w_ref, x_ref, o_ref):
    out_chan = o_ref.shape[1]
    cell_count = x_ref.shape[1]
    x = x_ref[...]
    cell = lax.broadcasted_iota(jnp.int32, (out_chan, cell_count), 1)
    row = lax.shift_right_logical(cell, W.bit_length() - 1)
    col = cell & (W - 1)
    rows = cell_count // W
    masks = []
    for kh in range(3):
        for kw in range(3):
            ok = None
            if kh == 0:
                ok = row >= 1
            elif kh == 2:
                ok = row < rows - 1
            if kw == 0:
                ok = (col >= 1) if ok is None else ok & (col >= 1)
            elif kw == 2:
                ok = (col < W - 1) if ok is None else ok & (col < W - 1)
            masks.append(ok)
    for kd in range(3):
        z = jnp.dot(w_ref[kd], x, preferred_element_type=jnp.float32)
        acc = None
        for kh in range(3):
            for kw in range(3):
                t = kh * 3 + kw
                shift = (kh - 1) * W + (kw - 1)
                zt = z[t * out_chan : (t + 1) * out_chan]
                if shift != 0:
                    zt = pltpu.roll(zt, (-shift) % cell_count, 1)
                if masks[t] is not None:
                    zt = jnp.where(masks[t], zt, 0.0)
                acc = zt if acc is None else acc + zt
        o_ref[kd] = acc


def plane_partials(wk, x):
    out_chan = wk.shape[1] // 9
    cell_count = x.shape[1]
    return pl.pallas_call(
        plane_kernel,
        out_shape=jax.ShapeDtypeStruct((3, out_chan, cell_count), jnp.float32),
        compiler_params=pltpu.CompilerParams(vmem_limit_bytes=48 * 1024 * 1024),
    )(wk, x)


def kernel_filters(filters):
    taps, in_chan, out_chan = filters.shape
    f = filters.reshape(3, 9, in_chan, out_chan).transpose(0, 1, 3, 2)
    return f.reshape(3, 9 * out_chan, in_chan)


def depth_combine(partials):
    peers = lax.axis_size("depth")
    up = [(i, i + 1) for i in range(peers - 1)]
    down = [(j, i) for i, j in up]
    from_below = lax.ppermute(partials[-1, 0], "depth", up)
    from_above = lax.ppermute(partials[0, 2], "depth", down)
    planes = partials.shape[0]
    lower = [from_below] + [partials[p - 1, 0] for p in range(1, planes)]
    upper = [partials[p + 1, 2] for p in range(planes - 1)] + [from_above]
    return jnp.stack([partials[p, 1] + lower[p] + upper[p] for p in range(planes)], 0)


def layer(wk, source):
    planes = source.shape[1]
    partials = jnp.stack([plane_partials(wk, source[:, p]) for p in range(planes)], 0)
    return depth_combine(partials)


CHAN = ("chip", "core")


def gather_chan(local):
    pair = lax.all_gather(local, "core", axis=0, tiled=True)
    n = lax.axis_size("chip")
    got = [pair] + [
        lax.ppermute(pair, "chip", [(i, (i + k) % n) for i in range(n)]) for k in range(1, n)
    ]
    return jnp.concatenate(got, 0)


def match_order(wk):
    n = lax.axis_size("chip")
    me = lax.axis_index("chip")
    order = (me - jnp.arange(n)) % n
    taps, rows, in_chan = wk.shape
    blocks = jnp.take(wk.reshape(taps, rows, n, in_chan // n), order, axis=2)
    return blocks.reshape(taps, rows, in_chan)


def body(volume, w_first, b_first, w_second, b_second):
    chan_local, slab_depth, cell_count = volume.shape
    taps, in_local, out_chan = w_first.shape
    peers = lax.axis_size(CHAN)
    out_local = out_chan // peers
    sent = w_first.reshape(3, 9, in_local, peers, out_local).transpose(3, 0, 1, 4, 2)
    got = lax.all_to_all(sent, CHAN, 0, 0, tiled=True)
    n = lax.axis_size("chip")
    order = (lax.axis_index("chip") - jnp.arange(n)) % n
    got = jnp.take(got.reshape(n, peers // n, 3, 9 * out_local, in_local), order, axis=0)
    w1k = got.transpose(2, 3, 0, 1, 4).reshape(3, 9 * out_local, peers * in_local)
    w2k = match_order(kernel_filters(w_second))
    full_volume = gather_chan(volume)
    first_sum = layer(w1k, full_volume)
    hidden = jnp.maximum(first_sum + b_first[None, :, None], 0.0).astype(jnp.bfloat16)
    hidden = hidden.transpose(1, 0, 2)
    full_hidden = gather_chan(hidden)
    second_sum = layer(w2k, full_hidden)
    block_out = (second_sum + b_second[None, :, None]).astype(jnp.bfloat16)
    return block_out.transpose(1, 0, 2)


def solution(mesh):
    depth, chan = mesh.devices.shape
    split = jax.sharding.Mesh(mesh.devices.reshape(depth, chan // 2, 2), ("depth",) + CHAN)
    in_specs = (
        P(CHAN, "depth", None),
        P(None, CHAN, None),
        P(CHAN),
        P(None, None, CHAN),
        P(CHAN),
    )
    out_specs = P(CHAN, "depth", None)
    return jax.shard_map(body, mesh=split, in_specs=in_specs, out_specs=out_specs, check_vma=False)
```

```python
import jax
import jax.numpy as jnp
from jax import lax
from jax.experimental import pallas as pl
from jax.experimental.pallas import tpu as pltpu
from jax.sharding import PartitionSpec as P

W = 64


def plane_kernel(w_ref, x_ref, o_ref):
    out_chan = o_ref.shape[1]
    cell_count = x_ref.shape[1]
    x = x_ref[...]
    cell = lax.broadcasted_iota(jnp.int32, (out_chan, cell_count), 1)
    row = lax.shift_right_logical(cell, W.bit_length() - 1)
    col = cell & (W - 1)
    rows = cell_count // W
    masks = []
    for kh in range(3):
        for kw in range(3):
            ok = None
            if kh == 0:
                ok = row >= 1
            elif kh == 2:
                ok = row < rows - 1
            if kw == 0:
                ok = (col >= 1) if ok is None else ok & (col >= 1)
            elif kw == 2:
                ok = (col < W - 1) if ok is None else ok & (col < W - 1)
            masks.append(ok)
    for kd in range(3):
        z = lax.dot_general(
            w_ref[kd], x, (((0,), (0,)), ((), ())), preferred_element_type=jnp.float32
        )
        acc = None
        for kh in range(3):
            for kw in range(3):
                t = kh * 3 + kw
                shift = (kh - 1) * W + (kw - 1)
                zt = z[t * out_chan : (t + 1) * out_chan]
                if shift != 0:
                    zt = pltpu.roll(zt, (-shift) % cell_count, 1)
                if masks[t] is not None:
                    zt = jnp.where(masks[t], zt, 0.0)
                acc = zt if acc is None else acc + zt
        o_ref[kd] = acc


def plane_partials(wk, x):
    out_chan = wk.shape[2] // 9
    cell_count = x.shape[1]
    return pl.pallas_call(
        plane_kernel,
        out_shape=jax.ShapeDtypeStruct((3, out_chan, cell_count), jnp.float32),
        compiler_params=pltpu.CompilerParams(vmem_limit_bytes=48 * 1024 * 1024),
    )(wk, x)


def kernel_filters(filters):
    taps, in_chan, out_chan = filters.shape
    f = filters.reshape(3, 9, in_chan, out_chan).transpose(0, 2, 1, 3)
    return f.reshape(3, in_chan, 9 * out_chan)


def depth_combine(partials):
    peers = lax.axis_size("depth")
    up = [(i, i + 1) for i in range(peers - 1)]
    down = [(j, i) for i, j in up]
    from_below = lax.ppermute(partials[-1, 0], "depth", up)
    from_above = lax.ppermute(partials[0, 2], "depth", down)
    planes = partials.shape[0]
    lower = [from_below] + [partials[p - 1, 0] for p in range(1, planes)]
    upper = [partials[p + 1, 2] for p in range(planes - 1)] + [from_above]
    return jnp.stack([partials[p, 1] + lower[p] + upper[p] for p in range(planes)], 0)


def layer(wk, planes):
    partials = jnp.stack([plane_partials(wk, plane) for plane in planes], 0)
    return depth_combine(partials)


CHAN = ("chip", "core")


def gather_chan(local):
    pair = lax.all_gather(local, "core", axis=0, tiled=True)
    n = lax.axis_size("chip")
    got = [pair] + [
        lax.ppermute(pair, "chip", [(i, (i + k) % n) for i in range(n)]) for k in range(1, n)
    ]
    return jnp.concatenate(got, 0)


def match_order(wk):
    n = lax.axis_size("chip")
    me = lax.axis_index("chip")
    order = (me - jnp.arange(n)) % n
    taps, in_chan, cols = wk.shape
    blocks = jnp.take(wk.reshape(taps, n, in_chan // n, cols), order, axis=1)
    return blocks.reshape(taps, in_chan, cols)


def body(volume, w_first, b_first, w_second, b_second):
    chan_local, slab_depth, cell_count = volume.shape
    taps, in_local, out_chan = w_first.shape
    peers = lax.axis_size(CHAN)
    out_local = out_chan // peers
    sent = w_first.reshape(3, 9, in_local, peers, out_local).transpose(3, 0, 2, 1, 4)
    got = lax.all_to_all(sent.reshape(peers, 3, in_local, 9 * out_local), CHAN, 0, 0, tiled=True)
    n = lax.axis_size("chip")
    order = (lax.axis_index("chip") - jnp.arange(n)) % n
    got = jnp.take(got.reshape(n, peers // n, 3, in_local, 9 * out_local), order, axis=0)
    w1k = got.transpose(2, 0, 1, 3, 4).reshape(3, peers * in_local, 9 * out_local)
    w2k = match_order(kernel_filters(w_second))
    first_sum = layer(w1k, [gather_chan(volume[:, p]) for p in range(slab_depth)])
    hidden = jnp.maximum(first_sum + b_first[None, :, None], 0.0).astype(jnp.bfloat16)
    second_sum = layer(w2k, [gather_chan(hidden[p]) for p in range(slab_depth)])
    block_out = (second_sum + b_second[None, :, None]).astype(jnp.bfloat16)
    return block_out.transpose(1, 0, 2)


def solution(mesh):
    depth, chan = mesh.devices.shape
    split = jax.sharding.Mesh(mesh.devices.reshape(depth, chan // 2, 2), ("depth",) + CHAN)
    in_specs = (
        P(CHAN, "depth", None),
        P(None, CHAN, None),
        P(CHAN),
        P(None, None, CHAN),
        P(CHAN),
    )
    out_specs = P(CHAN, "depth", None)
    return jax.shard_map(body, mesh=split, in_specs=in_specs, out_specs=out_specs, check_vma=False)
```

```python
import jax
import jax.numpy as jnp
from jax import lax
from jax.experimental import pallas as pl
from jax.experimental.pallas import tpu as pltpu
from jax.sharding import PartitionSpec as P

W = 64


def plane_kernel(w_ref, x_ref, o_ref):
    out_chan = o_ref.shape[1]
    cell_count = x_ref.shape[1]
    x = x_ref[...]
    cell = lax.broadcasted_iota(jnp.int32, (out_chan, cell_count), 1)
    row = lax.shift_right_logical(cell, W.bit_length() - 1)
    col = cell & (W - 1)
    rows = cell_count // W
    masks = []
    for kh in range(3):
        for kw in range(3):
            ok = None
            if kh == 0:
                ok = row >= 1
            elif kh == 2:
                ok = row < rows - 1
            if kw == 0:
                ok = (col >= 1) if ok is None else ok & (col >= 1)
            elif kw == 2:
                ok = (col < W - 1) if ok is None else ok & (col < W - 1)
            masks.append(ok)
    for kd in range(3):
        z = lax.dot_general(
            w_ref[kd], x, (((0,), (0,)), ((), ())), preferred_element_type=jnp.float32
        )
        acc = None
        for kh in range(3):
            for kw in range(3):
                t = kh * 3 + kw
                shift = (kh - 1) * W + (kw - 1)
                zt = z[t * out_chan : (t + 1) * out_chan]
                if shift != 0:
                    zt = pltpu.roll(zt, (-shift) % cell_count, 1)
                if masks[t] is not None:
                    zt = jnp.where(masks[t], zt, 0.0)
                acc = zt if acc is None else acc + zt
        o_ref[kd] = acc


def plane_partials(wk, x):
    out_chan = wk.shape[2] // 9
    cell_count = x.shape[1]
    return pl.pallas_call(
        plane_kernel,
        out_shape=jax.ShapeDtypeStruct((3, out_chan, cell_count), jnp.float32),
        compiler_params=pltpu.CompilerParams(vmem_limit_bytes=48 * 1024 * 1024),
    )(wk, x)


def kernel_filters(filters):
    taps, in_chan, out_chan = filters.shape
    f = filters.reshape(3, 9, in_chan, out_chan).transpose(0, 2, 1, 3)
    return f.reshape(3, in_chan, 9 * out_chan)


def depth_combine(partials):
    peers = lax.axis_size("depth")
    up = [(i, i + 1) for i in range(peers - 1)]
    down = [(j, i) for i, j in up]
    from_below = lax.ppermute(partials[-1, 0], "depth", up)
    from_above = lax.ppermute(partials[0, 2], "depth", down)
    planes = partials.shape[0]
    lower = [from_below] + [partials[p - 1, 0] for p in range(1, planes)]
    upper = [partials[p + 1, 2] for p in range(planes - 1)] + [from_above]
    return jnp.stack([partials[p, 1] + lower[p] + upper[p] for p in range(planes)], 0)


def layer(wk, planes):
    partials = jnp.stack([plane_partials(wk, plane) for plane in planes], 0)
    return depth_combine(partials)


CHAN = ("chip", "core")


def gather_chan(local):
    n = lax.axis_size("chip")
    got = [local] + [
        lax.ppermute(local, "chip", [(i, (i + k) % n) for i in range(n)]) for k in range(1, n)
    ]
    both = lax.all_gather(jnp.stack(got, 0), "core", axis=0)
    return both.reshape((-1,) + local.shape[1:])


def block_order():
    n = lax.axis_size("chip")
    return (lax.axis_index("chip") - jnp.arange(n)) % n


def match_order(wk):
    n = lax.axis_size("chip")
    taps, in_chan, cols = wk.shape
    blocks = jnp.take(wk.reshape(taps, n, 2, in_chan // (2 * n), cols), block_order(), axis=1)
    return blocks.transpose(0, 2, 1, 3, 4).reshape(taps, in_chan, cols)


def body(volume, w_first, b_first, w_second, b_second):
    chan_local, slab_depth, cell_count = volume.shape
    taps, in_local, out_chan = w_first.shape
    peers = lax.axis_size(CHAN)
    out_local = out_chan // peers
    sent = w_first.reshape(3, 9, in_local, peers, out_local).transpose(3, 0, 2, 1, 4)
    got = lax.all_to_all(sent.reshape(peers, 3, in_local, 9 * out_local), CHAN, 0, 0, tiled=True)
    n = lax.axis_size("chip")
    got = jnp.take(got.reshape(n, peers // n, 3, in_local, 9 * out_local), block_order(), axis=0)
    w1k = got.transpose(2, 1, 0, 3, 4).reshape(3, peers * in_local, 9 * out_local)
    w2k = match_order(kernel_filters(w_second))
    first_sum = layer(w1k, [gather_chan(volume[:, p]) for p in range(slab_depth)])
    hidden = jnp.maximum(first_sum + b_first[None, :, None], 0.0).astype(jnp.bfloat16)
    second_sum = layer(w2k, [gather_chan(hidden[p]) for p in range(slab_depth)])
    block_out = (second_sum + b_second[None, :, None]).astype(jnp.bfloat16)
    return block_out.transpose(1, 0, 2)


def solution(mesh):
    depth, chan = mesh.devices.shape
    split = jax.sharding.Mesh(mesh.devices.reshape(depth, chan // 2, 2), ("depth",) + CHAN)
    in_specs = (
        P(CHAN, "depth", None),
        P(None, CHAN, None),
        P(CHAN),
        P(None, None, CHAN),
        P(CHAN),
    )
    out_specs = P(CHAN, "depth", None)
    return jax.shard_map(body, mesh=split, in_specs=in_specs, out_specs=out_specs, check_vma=False)
```

```python
import jax
import jax.numpy as jnp
from jax import lax
from jax.experimental import pallas as pl
from jax.experimental.pallas import tpu as pltpu
from jax.sharding import PartitionSpec as P

W = 64


def plane_kernel(w_ref, x_ref, o_ref):
    out_chan = o_ref.shape[1]
    cell_count = x_ref.shape[1]
    x = x_ref[...]
    cell = lax.broadcasted_iota(jnp.int32, (out_chan, cell_count), 1)
    row = lax.shift_right_logical(cell, W.bit_length() - 1)
    col = cell & (W - 1)
    rows = cell_count // W
    masks = []
    for kh in range(3):
        for kw in range(3):
            ok = None
            if kh == 0:
                ok = row >= 1
            elif kh == 2:
                ok = row < rows - 1
            if kw == 0:
                ok = (col >= 1) if ok is None else ok & (col >= 1)
            elif kw == 2:
                ok = (col < W - 1) if ok is None else ok & (col < W - 1)
            masks.append(ok)
    for kd in range(3):
        z = lax.dot_general(
            w_ref[kd], x, (((0,), (0,)), ((), ())), preferred_element_type=jnp.float32
        )
        acc = None
        for kh in range(3):
            for kw in range(3):
                t = kh * 3 + kw
                shift = (kh - 1) * W + (kw - 1)
                zt = z[t * out_chan : (t + 1) * out_chan]
                if shift != 0:
                    zt = pltpu.roll(zt, (-shift) % cell_count, 1)
                if masks[t] is not None:
                    zt = jnp.where(masks[t], zt, 0.0)
                acc = zt if acc is None else acc + zt
        o_ref[kd] = acc


def plane_partials(wk, x):
    out_chan = wk.shape[2] // 9
    cell_count = x.shape[1]
    return pl.pallas_call(
        plane_kernel,
        out_shape=jax.ShapeDtypeStruct((3, out_chan, cell_count), jnp.float32),
        compiler_params=pltpu.CompilerParams(vmem_limit_bytes=48 * 1024 * 1024),
    )(wk, x)


def kernel_filters(filters):
    taps, in_chan, out_chan = filters.shape
    f = filters.reshape(3, 9, in_chan, out_chan).transpose(0, 2, 1, 3)
    return f.reshape(3, in_chan, 9 * out_chan)


def depth_combine(partials):
    peers = lax.axis_size("depth")
    up = [(i, i + 1) for i in range(peers - 1)]
    down = [(j, i) for i, j in up]
    from_below = lax.ppermute(partials[-1, 0], "depth", up)
    from_above = lax.ppermute(partials[0, 2], "depth", down)
    planes = partials.shape[0]
    lower = [from_below] + [partials[p - 1, 0] for p in range(1, planes)]
    upper = [partials[p + 1, 2] for p in range(planes - 1)] + [from_above]
    return jnp.stack([partials[p, 1] + lower[p] + upper[p] for p in range(planes)], 0)


def layer(wk, planes):
    partials = jnp.stack([plane_partials(wk, plane) for plane in planes], 0)
    return depth_combine(partials)


CHAN = ("chip", "core")


def gather_chan(local):
    n = lax.axis_size("chip")
    got = [local] + [
        lax.ppermute(local, "chip", [(i, (i + k) % n) for i in range(n)]) for k in range(1, n)
    ]
    mine = jnp.stack(got, 0)
    other = lax.ppermute(mine, "core", [(0, 1), (1, 0)])
    return jnp.concatenate([mine, other], 0).reshape((-1,) + local.shape[1:])


def block_order():
    n = lax.axis_size("chip")
    return (lax.axis_index("chip") - jnp.arange(n)) % n


def core_order():
    return (lax.axis_index("core") + jnp.arange(2)) % 2


def match_order(wk):
    n = lax.axis_size("chip")
    taps, in_chan, cols = wk.shape
    blocks = jnp.take(wk.reshape(taps, n, 2, in_chan // (2 * n), cols), block_order(), axis=1)
    blocks = jnp.take(blocks, core_order(), axis=2)
    return blocks.transpose(0, 2, 1, 3, 4).reshape(taps, in_chan, cols)


def body(volume, w_first, b_first, w_second, b_second):
    chan_local, slab_depth, cell_count = volume.shape
    taps, in_local, out_chan = w_first.shape
    peers = lax.axis_size(CHAN)
    out_local = out_chan // peers
    sent = w_first.reshape(3, 9, in_local, peers, out_local).transpose(3, 0, 2, 1, 4)
    got = lax.all_to_all(sent.reshape(peers, 3, in_local, 9 * out_local), CHAN, 0, 0, tiled=True)
    n = lax.axis_size("chip")
    got = jnp.take(got.reshape(n, peers // n, 3, in_local, 9 * out_local), block_order(), axis=0)
    got = jnp.take(got, core_order(), axis=1)
    w1k = got.transpose(2, 1, 0, 3, 4).reshape(3, peers * in_local, 9 * out_local)
    w2k = match_order(kernel_filters(w_second))
    first_sum = layer(w1k, [gather_chan(volume[:, p]) for p in range(slab_depth)])
    hidden = jnp.maximum(first_sum + b_first[None, :, None], 0.0).astype(jnp.bfloat16)
    second_sum = layer(w2k, [gather_chan(hidden[p]) for p in range(slab_depth)])
    block_out = (second_sum + b_second[None, :, None]).astype(jnp.bfloat16)
    return block_out.transpose(1, 0, 2)


def solution(mesh):
    depth, chan = mesh.devices.shape
    split = jax.sharding.Mesh(mesh.devices.reshape(depth, chan // 2, 2), ("depth",) + CHAN)
    in_specs = (
        P(CHAN, "depth", None),
        P(None, CHAN, None),
        P(CHAN),
        P(None, None, CHAN),
        P(CHAN),
    )
    out_specs = P(CHAN, "depth", None)
    return jax.shard_map(body, mesh=split, in_specs=in_specs, out_specs=out_specs, check_vma=False)
```

```python
import jax
import jax.numpy as jnp
from jax import lax
from jax.experimental import pallas as pl
from jax.experimental.pallas import tpu as pltpu
from jax.sharding import PartitionSpec as P

W = 64


def plane_kernel(w_ref, *refs):
    *x_refs, o_ref = refs
    out_chan = o_ref.shape[1]
    cell_count = x_refs[0].shape[1]
    x = jnp.concatenate([r[...] for r in x_refs], 0)
    cell = lax.broadcasted_iota(jnp.int32, (out_chan, cell_count), 1)
    row = lax.shift_right_logical(cell, W.bit_length() - 1)
    col = cell & (W - 1)
    rows = cell_count // W
    masks = []
    for kh in range(3):
        for kw in range(3):
            ok = None
            if kh == 0:
                ok = row >= 1
            elif kh == 2:
                ok = row < rows - 1
            if kw == 0:
                ok = (col >= 1) if ok is None else ok & (col >= 1)
            elif kw == 2:
                ok = (col < W - 1) if ok is None else ok & (col < W - 1)
            masks.append(ok)
    for kd in range(3):
        z = lax.dot_general(
            w_ref[kd], x, (((0,), (0,)), ((), ())), preferred_element_type=jnp.float32
        )
        acc = None
        for kh in range(3):
            for kw in range(3):
                t = kh * 3 + kw
                shift = (kh - 1) * W + (kw - 1)
                zt = z[t * out_chan : (t + 1) * out_chan]
                if shift != 0:
                    zt = pltpu.roll(zt, (-shift) % cell_count, 1)
                if masks[t] is not None:
                    zt = jnp.where(masks[t], zt, 0.0)
                acc = zt if acc is None else acc + zt
        o_ref[kd] = acc


def plane_partials(wk, pieces):
    out_chan = wk.shape[2] // 9
    cell_count = pieces[0].shape[1]
    return pl.pallas_call(
        plane_kernel,
        out_shape=jax.ShapeDtypeStruct((3, out_chan, cell_count), jnp.float32),
        compiler_params=pltpu.CompilerParams(vmem_limit_bytes=48 * 1024 * 1024),
    )(wk, *pieces)


def kernel_filters(filters):
    taps, in_chan, out_chan = filters.shape
    f = filters.reshape(3, 9, in_chan, out_chan).transpose(0, 2, 1, 3)
    return f.reshape(3, in_chan, 9 * out_chan)


def depth_combine(partials):
    peers = lax.axis_size("depth")
    up = [(i, i + 1) for i in range(peers - 1)]
    down = [(j, i) for i, j in up]
    from_below = lax.ppermute(partials[-1, 0], "depth", up)
    from_above = lax.ppermute(partials[0, 2], "depth", down)
    planes = partials.shape[0]
    lower = [from_below] + [partials[p - 1, 0] for p in range(1, planes)]
    upper = [partials[p + 1, 2] for p in range(planes - 1)] + [from_above]
    return jnp.stack([partials[p, 1] + lower[p] + upper[p] for p in range(planes)], 0)


def layer(wk, planes, carry=None):
    partials = jnp.stack([plane_partials(wk, plane) for plane in planes], 0)
    partials, carry = lax.optimization_barrier((partials, carry))
    return depth_combine(partials), carry


CHAN = ("chip", "core")


def gather_chan(local):
    n = lax.axis_size("chip")
    got = [local] + [
        lax.ppermute(local, "chip", [(i, (i + k) % n) for i in range(n)]) for k in range(1, n)
    ]
    swap = [(0, 1), (1, 0)]
    return got + [lax.ppermute(piece, "core", swap) for piece in got]


def block_order():
    n = lax.axis_size("chip")
    return (lax.axis_index("chip") - jnp.arange(n)) % n


def core_order():
    return (lax.axis_index("core") + jnp.arange(2)) % 2


def match_order(wk):
    n = lax.axis_size("chip")
    taps, in_chan, cols = wk.shape
    blocks = jnp.take(wk.reshape(taps, n, 2, in_chan // (2 * n), cols), block_order(), axis=1)
    blocks = jnp.take(blocks, core_order(), axis=2)
    return blocks.transpose(0, 2, 1, 3, 4).reshape(taps, in_chan, cols)


def body(volume, w_first, b_first, w_second, b_second):
    chan_local, slab_depth, cell_count = volume.shape
    taps, in_local, out_chan = w_first.shape
    peers = lax.axis_size(CHAN)
    out_local = out_chan // peers
    sent = w_first.reshape(3, 9, in_local, peers, out_local).transpose(3, 0, 2, 1, 4)
    got = lax.all_to_all(sent.reshape(peers, 3, in_local, 9 * out_local), CHAN, 0, 0, tiled=True)
    n = lax.axis_size("chip")
    got = jnp.take(got.reshape(n, peers // n, 3, in_local, 9 * out_local), block_order(), axis=0)
    got = jnp.take(got, core_order(), axis=1)
    w1k = got.transpose(2, 1, 0, 3, 4).reshape(3, peers * in_local, 9 * out_local)
    first_sum, w_second = layer(
        w1k, [gather_chan(volume[:, p]) for p in range(slab_depth)], w_second
    )
    w2k = match_order(kernel_filters(w_second))
    hidden = jnp.maximum(first_sum + b_first[None, :, None], 0.0).astype(jnp.bfloat16)
    second_sum, _ = layer(w2k, [gather_chan(hidden[p]) for p in range(slab_depth)])
    block_out = (second_sum + b_second[None, :, None]).astype(jnp.bfloat16)
    return block_out.transpose(1, 0, 2)


def solution(mesh):
    depth, chan = mesh.devices.shape
    split = jax.sharding.Mesh(mesh.devices.reshape(depth, chan // 2, 2), ("depth",) + CHAN)
    in_specs = (
        P(CHAN, "depth", None),
        P(None, CHAN, None),
        P(CHAN),
        P(None, None, CHAN),
        P(CHAN),
    )
    out_specs = P(CHAN, "depth", None)
    return jax.shard_map(body, mesh=split, in_specs=in_specs, out_specs=out_specs, check_vma=False)
```

```python
import jax
import jax.numpy as jnp
from jax import lax
from jax.experimental import pallas as pl
from jax.experimental.pallas import tpu as pltpu
from jax.sharding import PartitionSpec as P

W = 64


def plane_kernel(w_ref, *refs):
    *x_refs, o_ref = refs
    out_chan = o_ref.shape[1]
    cell_count = x_refs[0].shape[1]
    x = jnp.concatenate([r[...] for r in x_refs], 0)
    cell = lax.broadcasted_iota(jnp.int32, (out_chan, cell_count), 1)
    row = lax.shift_right_logical(cell, W.bit_length() - 1)
    col = cell & (W - 1)
    rows = cell_count // W
    masks = []
    for kh in range(3):
        for kw in range(3):
            ok = None
            if kh == 0:
                ok = row >= 1
            elif kh == 2:
                ok = row < rows - 1
            if kw == 0:
                ok = (col >= 1) if ok is None else ok & (col >= 1)
            elif kw == 2:
                ok = (col < W - 1) if ok is None else ok & (col < W - 1)
            masks.append(ok)
    for kd in range(3):
        z = lax.dot_general(
            w_ref[kd], x, (((0,), (0,)), ((), ())), preferred_element_type=jnp.float32
        )
        acc = None
        for kh in range(3):
            for kw in range(3):
                t = kh * 3 + kw
                shift = (kh - 1) * W + (kw - 1)
                zt = z[t * out_chan : (t + 1) * out_chan]
                if shift != 0:
                    zt = pltpu.roll(zt, (-shift) % cell_count, 1)
                if masks[t] is not None:
                    zt = jnp.where(masks[t], zt, 0.0)
                acc = zt if acc is None else acc + zt
        o_ref[kd] = acc


def prep_kernel(w_ref, o_ref):
    dests, _, c_in, lanes = o_ref.shape
    out_local = w_ref.shape[2] // dests
    width = max(lanes, w_ref.shape[2])
    lane = lax.broadcasted_iota(jnp.int32, (c_in, width), 1)
    pad = width - w_ref.shape[2]
    for kd in range(3):
        rows = [w_ref[kd * 9 + t].astype(jnp.float32) for t in range(9)]
        if pad:
            rows = [jnp.concatenate([r, jnp.zeros((c_in, pad), r.dtype)], 1) for r in rows]
        for dest in range(dests):
            acc = jnp.zeros((c_in, width), jnp.float32)
            for t in range(9):
                shift = (t - dest) * out_local % width
                moved = pltpu.roll(rows[t], shift, 1) if shift else rows[t]
                ok = (lane >= t * out_local) & (lane < (t + 1) * out_local)
                acc = jnp.where(ok, moved, acc)
            o_ref[dest, kd] = acc[:, :lanes].astype(o_ref.dtype)


def per_destination(w_first, dests):
    taps, c_in, out_chan = w_first.shape
    lanes = (9 * (out_chan // dests) + 127) // 128 * 128
    return pl.pallas_call(
        prep_kernel,
        out_shape=jax.ShapeDtypeStruct((dests, 3, c_in, lanes), w_first.dtype),
    )(w_first)


def plane_partials(wk, pieces):
    out_chan = wk.shape[2] // 9
    cell_count = pieces[0].shape[1]
    return pl.pallas_call(
        plane_kernel,
        out_shape=jax.ShapeDtypeStruct((3, out_chan, cell_count), jnp.float32),
        compiler_params=pltpu.CompilerParams(vmem_limit_bytes=48 * 1024 * 1024),
    )(wk, *pieces)


def kernel_filters(filters):
    taps, in_chan, out_chan = filters.shape
    f = filters.reshape(3, 9, in_chan, out_chan).transpose(0, 2, 1, 3)
    return f.reshape(3, in_chan, 9 * out_chan)


def depth_combine(partials):
    peers = lax.axis_size("depth")
    up = [(i, i + 1) for i in range(peers - 1)]
    down = [(j, i) for i, j in up]
    from_below = lax.ppermute(partials[-1, 0], "depth", up)
    from_above = lax.ppermute(partials[0, 2], "depth", down)
    planes = partials.shape[0]
    lower = [from_below] + [partials[p - 1, 0] for p in range(1, planes)]
    upper = [partials[p + 1, 2] for p in range(planes - 1)] + [from_above]
    return jnp.stack([partials[p, 1] + lower[p] + upper[p] for p in range(planes)], 0)


def layer(wk, planes, carry=None):
    partials = jnp.stack([plane_partials(wk, plane) for plane in planes], 0)
    partials, carry = lax.optimization_barrier((partials, carry))
    return depth_combine(partials), carry


CHAN = ("chip", "core")


def gather_chan(local):
    n = lax.axis_size("chip")
    got = [local] + [
        lax.ppermute(local, "chip", [(i, (i + k) % n) for i in range(n)]) for k in range(1, n)
    ]
    swap = [(0, 1), (1, 0)]
    return got + [lax.ppermute(piece, "core", swap) for piece in got]


def block_order():
    n = lax.axis_size("chip")
    return (lax.axis_index("chip") - jnp.arange(n)) % n


def core_order():
    return (lax.axis_index("core") + jnp.arange(2)) % 2


def match_order(wk):
    n = lax.axis_size("chip")
    taps, in_chan, cols = wk.shape
    blocks = jnp.take(wk.reshape(taps, n, 2, in_chan // (2 * n), cols), block_order(), axis=1)
    blocks = jnp.take(blocks, core_order(), axis=2)
    return blocks.transpose(0, 2, 1, 3, 4).reshape(taps, in_chan, cols)


def body(volume, w_first, b_first, w_second, b_second):
    chan_local, slab_depth, cell_count = volume.shape
    taps, in_local, out_chan = w_first.shape
    peers = lax.axis_size(CHAN)
    out_local = out_chan // peers
    sent = per_destination(w_first, peers)
    got = lax.all_to_all(sent, CHAN, 0, 0, tiled=True)
    n = lax.axis_size("chip")
    got = jnp.take(got.reshape((n, peers // n) + got.shape[1:]), block_order(), axis=0)
    got = jnp.take(got, core_order(), axis=1)[..., : 9 * out_local]
    w1k = got.transpose(2, 1, 0, 3, 4).reshape(3, peers * in_local, 9 * out_local)
    first_sum, w_second = layer(
        w1k, [gather_chan(volume[:, p]) for p in range(slab_depth)], w_second
    )
    w2k = match_order(kernel_filters(w_second))
    hidden = jnp.maximum(first_sum + b_first[None, :, None], 0.0).astype(jnp.bfloat16)
    second_sum, _ = layer(w2k, [gather_chan(hidden[p]) for p in range(slab_depth)])
    block_out = (second_sum + b_second[None, :, None]).astype(jnp.bfloat16)
    return block_out.transpose(1, 0, 2)


def solution(mesh):
    depth, chan = mesh.devices.shape
    split = jax.sharding.Mesh(mesh.devices.reshape(depth, chan // 2, 2), ("depth",) + CHAN)
    in_specs = (
        P(CHAN, "depth", None),
        P(None, CHAN, None),
        P(CHAN),
        P(None, None, CHAN),
        P(CHAN),
    )
    out_specs = P(CHAN, "depth", None)
    return jax.shard_map(body, mesh=split, in_specs=in_specs, out_specs=out_specs, check_vma=False)
```

```python
import jax
import jax.numpy as jnp
from jax import lax
from jax.experimental import pallas as pl
from jax.experimental.pallas import tpu as pltpu
from jax.sharding import PartitionSpec as P

W = 64


def plane_kernel(w_ref, *refs):
    *x_refs, o_ref = refs
    out_chan = o_ref.shape[1]
    cell_count = x_refs[0].shape[1]
    x = jnp.concatenate([r[...] for r in x_refs], 0)
    cell = lax.broadcasted_iota(jnp.int32, (out_chan, cell_count), 1)
    row = lax.shift_right_logical(cell, W.bit_length() - 1)
    col = cell & (W - 1)
    rows = cell_count // W
    masks = []
    for kh in range(3):
        for kw in range(3):
            ok = None
            if kh == 0:
                ok = row >= 1
            elif kh == 2:
                ok = row < rows - 1
            if kw == 0:
                ok = (col >= 1) if ok is None else ok & (col >= 1)
            elif kw == 2:
                ok = (col < W - 1) if ok is None else ok & (col < W - 1)
            masks.append(ok)
    for kd in range(3):
        z = lax.dot_general(
            w_ref[kd], x, (((0,), (0,)), ((), ())), preferred_element_type=jnp.float32
        )
        acc = None
        for kh in range(3):
            for kw in range(3):
                t = kh * 3 + kw
                shift = (kh - 1) * W + (kw - 1)
                zt = z[t * out_chan : (t + 1) * out_chan]
                if shift != 0:
                    zt = pltpu.roll(zt, (-shift) % cell_count, 1)
                if masks[t] is not None:
                    zt = jnp.where(masks[t], zt, 0.0)
                acc = zt if acc is None else acc + zt
        o_ref[kd] = acc


def prep_kernel(w_ref, o_ref):
    dests, _, c_in, lanes = o_ref.shape
    out_local = w_ref.shape[2] // dests
    width = max(lanes, w_ref.shape[2])
    lane = lax.broadcasted_iota(jnp.int32, (c_in, width), 1)
    pad = width - w_ref.shape[2]
    for kd in range(3):
        rows = [w_ref[kd * 9 + t].astype(jnp.float32) for t in range(9)]
        if pad:
            rows = [jnp.concatenate([r, jnp.zeros((c_in, pad), r.dtype)], 1) for r in rows]
        for dest in range(dests):
            acc = jnp.zeros((c_in, width), jnp.float32)
            for t in range(9):
                shift = (t - dest) * out_local % width
                moved = pltpu.roll(rows[t], shift, 1) if shift else rows[t]
                ok = (lane >= t * out_local) & (lane < (t + 1) * out_local)
                acc = jnp.where(ok, moved, acc)
            o_ref[dest, kd] = acc[:, :lanes].astype(o_ref.dtype)


def per_destination(w_first, dests):
    taps, c_in, out_chan = w_first.shape
    lanes = 9 * (out_chan // dests)
    return pl.pallas_call(
        prep_kernel,
        out_shape=jax.ShapeDtypeStruct((dests, 3, c_in, lanes), w_first.dtype),
    )(w_first)


def plane_partials(wk, pieces):
    out_chan = wk.shape[2] // 9
    cell_count = pieces[0].shape[1]
    return pl.pallas_call(
        plane_kernel,
        out_shape=jax.ShapeDtypeStruct((3, out_chan, cell_count), jnp.float32),
        compiler_params=pltpu.CompilerParams(vmem_limit_bytes=48 * 1024 * 1024),
    )(wk, *pieces)


def kernel_filters(filters):
    taps, in_chan, out_chan = filters.shape
    f = filters.reshape(3, 9, in_chan, out_chan).transpose(0, 2, 1, 3)
    return f.reshape(3, in_chan, 9 * out_chan)


def depth_combine(partials):
    peers = lax.axis_size("depth")
    up = [(i, i + 1) for i in range(peers - 1)]
    down = [(j, i) for i, j in up]
    from_below = lax.ppermute(partials[-1, 0], "depth", up)
    from_above = lax.ppermute(partials[0, 2], "depth", down)
    planes = partials.shape[0]
    lower = [from_below] + [partials[p - 1, 0] for p in range(1, planes)]
    upper = [partials[p + 1, 2] for p in range(planes - 1)] + [from_above]
    return jnp.stack([partials[p, 1] + lower[p] + upper[p] for p in range(planes)], 0)


def layer(wk, planes, carry=None):
    partials = jnp.stack([plane_partials(wk, plane) for plane in planes], 0)
    partials, carry = lax.optimization_barrier((partials, carry))
    return depth_combine(partials), carry


CHAN = ("chip", "core")


def gather_chan(local):
    n = lax.axis_size("chip")
    got = [local] + [
        lax.ppermute(local, "chip", [(i, (i + k) % n) for i in range(n)]) for k in range(1, n)
    ]
    swap = [(0, 1), (1, 0)]
    return got + [lax.ppermute(piece, "core", swap) for piece in got]


def block_order():
    n = lax.axis_size("chip")
    return (lax.axis_index("chip") - jnp.arange(n)) % n


def core_order():
    return (lax.axis_index("core") + jnp.arange(2)) % 2


def match_order(wk):
    n = lax.axis_size("chip")
    taps, in_chan, cols = wk.shape
    blocks = jnp.take(wk.reshape(taps, n, 2, in_chan // (2 * n), cols), block_order(), axis=1)
    blocks = jnp.take(blocks, core_order(), axis=2)
    return blocks.transpose(0, 2, 1, 3, 4).reshape(taps, in_chan, cols)


def body(volume, w_first, b_first, w_second, b_second):
    chan_local, slab_depth, cell_count = volume.shape
    taps, in_local, out_chan = w_first.shape
    peers = lax.axis_size(CHAN)
    out_local = out_chan // peers
    sent = per_destination(w_first, peers)
    got = lax.all_to_all(sent, CHAN, 0, 0, tiled=True)
    n = lax.axis_size("chip")
    got = jnp.take(got.reshape((n, peers // n) + got.shape[1:]), block_order(), axis=0)
    got = jnp.take(got, core_order(), axis=1)
    w1k = got.transpose(2, 1, 0, 3, 4).reshape(3, peers * in_local, 9 * out_local)
    first_sum, w_second = layer(
        w1k, [gather_chan(volume[:, p]) for p in range(slab_depth)], w_second
    )
    w2k = match_order(kernel_filters(w_second))
    hidden = jnp.maximum(first_sum + b_first[None, :, None], 0.0).astype(jnp.bfloat16)
    second_sum, _ = layer(w2k, [gather_chan(hidden[p]) for p in range(slab_depth)])
    block_out = (second_sum + b_second[None, :, None]).astype(jnp.bfloat16)
    return block_out.transpose(1, 0, 2)


def solution(mesh):
    depth, chan = mesh.devices.shape
    split = jax.sharding.Mesh(mesh.devices.reshape(depth, chan // 2, 2), ("depth",) + CHAN)
    in_specs = (
        P(CHAN, "depth", None),
        P(None, CHAN, None),
        P(CHAN),
        P(None, None, CHAN),
        P(CHAN),
    )
    out_specs = P(CHAN, "depth", None)
    return jax.shard_map(body, mesh=split, in_specs=in_specs, out_specs=out_specs, check_vma=False)
```

```python
import jax
import jax.numpy as jnp
from jax import lax
from jax.experimental import pallas as pl
from jax.experimental.pallas import tpu as pltpu
from jax.sharding import PartitionSpec as P


W = 64


def plane_kernel(w_ref, *refs):
    *x_refs, o_ref = refs
    out_chan = o_ref.shape[1]
    cell_count = x_refs[0].shape[1]
    x = jnp.concatenate([r[...] for r in x_refs], 0)
    cell = lax.broadcasted_iota(jnp.int32, (out_chan, cell_count), 1)
    row = lax.shift_right_logical(cell, W.bit_length() - 1)
    col = cell & (W - 1)
    rows = cell_count // W
    masks = []
    for kh in range(3):
        for kw in range(3):
            ok = None
            if kh == 0:
                ok = row >= 1
            elif kh == 2:
                ok = row < rows - 1
            if kw == 0:
                ok = (col >= 1) if ok is None else ok & (col >= 1)
            elif kw == 2:
                ok = (col < W - 1) if ok is None else ok & (col < W - 1)
            masks.append(ok)
    for kd in range(3):
        z = lax.dot_general(
            w_ref[kd], x, (((0,), (0,)), ((), ())), preferred_element_type=jnp.float32
        )
        acc = None
        for kh in range(3):
            for kw in range(3):
                t = kh * 3 + kw
                shift = (kh - 1) * W + (kw - 1)
                zt = z[t * out_chan : (t + 1) * out_chan]
                if shift != 0:
                    zt = pltpu.roll(zt, (-shift) % cell_count, 1)
                if masks[t] is not None:
                    zt = jnp.where(masks[t], zt, 0.0)
                acc = zt if acc is None else acc + zt
        o_ref[kd] = acc


def prep_kernel(w_ref, o_ref):
    dests, _, c_in, lanes = o_ref.shape
    out_local = w_ref.shape[2] // dests
    width = max(lanes, w_ref.shape[2])
    lane = lax.broadcasted_iota(jnp.int32, (c_in, width), 1)
    pad = width - w_ref.shape[2]
    for kd in range(3):
        rows = [w_ref[kd * 9 + t].astype(jnp.float32) for t in range(9)]
        if pad:
            rows = [jnp.concatenate([r, jnp.zeros((c_in, pad), r.dtype)], 1) for r in rows]
        for dest in range(dests):
            acc = jnp.zeros((c_in, width), jnp.float32)
            for t in range(9):
                shift = (t - dest) * out_local % width
                moved = pltpu.roll(rows[t], shift, 1) if shift else rows[t]
                ok = (lane >= t * out_local) & (lane < (t + 1) * out_local)
                acc = jnp.where(ok, moved, acc)
            o_ref[dest, kd] = acc[:, :lanes].astype(o_ref.dtype)


def per_destination(w_first, dests):
    _, c_in, out_chan = w_first.shape
    lanes = 9 * (out_chan // dests)
    return pl.pallas_call(
        prep_kernel,
        out_shape=jax.ShapeDtypeStruct((dests, 3, c_in, lanes), w_first.dtype),
    )(w_first)


def plane_partials(wk, pieces):
    out_chan = wk.shape[2] // 9
    cell_count = pieces[0].shape[1]
    return pl.pallas_call(
        plane_kernel,
        out_shape=jax.ShapeDtypeStruct((3, out_chan, cell_count), jnp.float32),
        compiler_params=pltpu.CompilerParams(vmem_limit_bytes=48 * 1024 * 1024),
    )(wk, *pieces)


def kernel_filters(filters):
    _, in_chan, out_chan = filters.shape
    f = filters.reshape(3, 9, in_chan, out_chan).transpose(0, 2, 1, 3)
    return f.reshape(3, in_chan, 9 * out_chan)


def depth_combine(partials):
    peers = lax.axis_size("depth")
    up = [(i, i + 1) for i in range(peers - 1)]
    down = [(j, i) for i, j in up]
    from_below = lax.ppermute(partials[-1, 0], "depth", up)
    from_above = lax.ppermute(partials[0, 2], "depth", down)
    planes = partials.shape[0]
    lower = [from_below] + [partials[p - 1, 0] for p in range(1, planes)]
    upper = [partials[p + 1, 2] for p in range(planes - 1)] + [from_above]
    return jnp.stack([partials[p, 1] + lower[p] + upper[p] for p in range(planes)], 0)


def layer(wk, planes, carry=None):
    partials = jnp.stack([plane_partials(wk, plane) for plane in planes], 0)
    partials, carry = lax.optimization_barrier((partials, carry))
    return depth_combine(partials), carry


CHAN = ("chip", "core")


def gather_chan(local):
    n = lax.axis_size("chip")
    got = [local] + [
        lax.ppermute(local, "chip", [(i, (i + k) % n) for i in range(n)]) for k in range(1, n)
    ]
    swap = [(0, 1), (1, 0)]
    return got + [lax.ppermute(piece, "core", swap) for piece in got]


def block_order():
    n = lax.axis_size("chip")
    return (lax.axis_index("chip") - jnp.arange(n)) % n


def core_order():
    return (lax.axis_index("core") + jnp.arange(2)) % 2


def match_order(wk):
    n = lax.axis_size("chip")
    taps, in_chan, cols = wk.shape
    blocks = jnp.take(wk.reshape(taps, n, 2, in_chan // (2 * n), cols), block_order(), axis=1)
    blocks = jnp.take(blocks, core_order(), axis=2)
    return blocks.transpose(0, 2, 1, 3, 4).reshape(taps, in_chan, cols)


def block(volume, w_first, b_first, w_second, b_second):
    _, slab_depth, _ = volume.shape
    _, in_local, out_chan = w_first.shape
    peers = lax.axis_size(CHAN)
    out_local = out_chan // peers
    sent = per_destination(w_first, peers)
    got = lax.all_to_all(sent, CHAN, 0, 0, tiled=True)
    n = lax.axis_size("chip")
    got = jnp.take(got.reshape((n, peers // n) + got.shape[1:]), block_order(), axis=0)
    got = jnp.take(got, core_order(), axis=1)
    w1k = got.transpose(2, 1, 0, 3, 4).reshape(3, peers * in_local, 9 * out_local)
    first_sum, w_second = layer(
        w1k, [gather_chan(volume[:, p]) for p in range(slab_depth)], w_second
    )
    w2k = match_order(kernel_filters(w_second))
    hidden = jnp.maximum(first_sum + b_first[None, :, None], 0.0).astype(jnp.bfloat16)
    second_sum, _ = layer(w2k, [gather_chan(hidden[p]) for p in range(slab_depth)])
    block_out = (second_sum + b_second[None, :, None]).astype(jnp.bfloat16)
    return block_out.transpose(1, 0, 2)


def solution(mesh):
    depth, chan = mesh.devices.shape
    split = jax.sharding.Mesh(mesh.devices.reshape(depth, chan // 2, 2), ("depth",) + CHAN)
    in_specs = (
        P(CHAN, "depth", None),
        P(None, CHAN, None),
        P(CHAN),
        P(None, None, CHAN),
        P(CHAN),
    )
    out_specs = P(CHAN, "depth", None)
    return jax.shard_map(block, mesh=split, in_specs=in_specs, out_specs=out_specs, check_vma=False)
```

```python
import jax
import jax.numpy as jnp
from jax import lax
from jax.experimental import pallas as pl
from jax.experimental.pallas import tpu as pltpu
from jax.sharding import PartitionSpec as P

W = 64


def plane_kernel(w_ref, *refs):
    *x_refs, o0_ref, o1_ref, o2_ref = refs
    out_refs = (o0_ref, o1_ref, o2_ref)
    out_chan = o0_ref.shape[0]
    cell_count = x_refs[0].shape[1]
    x = jnp.concatenate([r[...] for r in x_refs], 0)
    cell = lax.broadcasted_iota(jnp.int32, (out_chan, cell_count), 1)
    row = lax.shift_right_logical(cell, W.bit_length() - 1)
    col = cell & (W - 1)
    rows = cell_count // W
    masks = []
    for kh in range(3):
        for kw in range(3):
            ok = None
            if kh == 0:
                ok = row >= 1
            elif kh == 2:
                ok = row < rows - 1
            if kw == 0:
                ok = (col >= 1) if ok is None else ok & (col >= 1)
            elif kw == 2:
                ok = (col < W - 1) if ok is None else ok & (col < W - 1)
            masks.append(ok)
    for kd in range(3):
        z = lax.dot_general(
            w_ref[kd], x, (((0,), (0,)), ((), ())), preferred_element_type=jnp.float32
        )
        acc = None
        for kh in range(3):
            for kw in range(3):
                t = kh * 3 + kw
                shift = (kh - 1) * W + (kw - 1)
                zt = z[t * out_chan : (t + 1) * out_chan]
                if shift != 0:
                    zt = pltpu.roll(zt, (-shift) % cell_count, 1)
                if masks[t] is not None:
                    zt = jnp.where(masks[t], zt, 0.0)
                acc = zt if acc is None else acc + zt
        out_refs[kd][...] = acc


def prep_kernel(w_ref, o_ref):
    dests, _, c_in, lanes = o_ref.shape
    out_local = w_ref.shape[2] // dests
    width = max(lanes, w_ref.shape[2])
    lane = lax.broadcasted_iota(jnp.int32, (c_in, width), 1)
    pad = width - w_ref.shape[2]
    for kd in range(3):
        rows = [w_ref[kd * 9 + t].astype(jnp.float32) for t in range(9)]
        if pad:
            rows = [jnp.concatenate([r, jnp.zeros((c_in, pad), r.dtype)], 1) for r in rows]
        for dest in range(dests):
            acc = jnp.zeros((c_in, width), jnp.float32)
            for t in range(9):
                shift = (t - dest) * out_local % width
                moved = pltpu.roll(rows[t], shift, 1) if shift else rows[t]
                ok = (lane >= t * out_local) & (lane < (t + 1) * out_local)
                acc = jnp.where(ok, moved, acc)
            o_ref[dest, kd] = acc[:, :lanes].astype(o_ref.dtype)


def per_destination(w_first, dests):
    taps, c_in, out_chan = w_first.shape
    lanes = 9 * (out_chan // dests)
    return pl.pallas_call(
        prep_kernel,
        out_shape=jax.ShapeDtypeStruct((dests, 3, c_in, lanes), w_first.dtype),
    )(w_first)


def plane_partials(wk, pieces):
    out_chan = wk.shape[2] // 9
    cell_count = pieces[0].shape[1]
    return pl.pallas_call(
        plane_kernel,
        out_shape=[jax.ShapeDtypeStruct((out_chan, cell_count), jnp.float32)] * 3,
        compiler_params=pltpu.CompilerParams(vmem_limit_bytes=48 * 1024 * 1024),
    )(wk, *pieces)


def kernel_filters(filters):
    taps, in_chan, out_chan = filters.shape
    f = filters.reshape(3, 9, in_chan, out_chan).transpose(0, 2, 1, 3)
    return f.reshape(3, in_chan, 9 * out_chan)


def depth_combine(partials):
    peers = lax.axis_size("depth")
    up = [(i, i + 1) for i in range(peers - 1)]
    down = [(j, i) for i, j in up]
    from_below = lax.ppermute(partials[-1][0], "depth", up)
    from_above = lax.ppermute(partials[0][2], "depth", down)
    planes = len(partials)
    lower = [from_below] + [partials[p - 1][0] for p in range(1, planes)]
    upper = [partials[p + 1][2] for p in range(planes - 1)] + [from_above]
    return jnp.stack([partials[p][1] + lower[p] + upper[p] for p in range(planes)], 0)


def layer(wk, planes, carry=None):
    partials = [tuple(plane_partials(wk, plane)) for plane in planes]
    partials, carry = lax.optimization_barrier((partials, carry))
    return depth_combine(partials), carry


CHAN = ("chip", "core")


def gather_chan(local):
    n = lax.axis_size("chip")
    got = [local] + [
        lax.ppermute(local, "chip", [(i, (i + k) % n) for i in range(n)]) for k in range(1, n)
    ]
    swap = [(0, 1), (1, 0)]
    return got + [lax.ppermute(piece, "core", swap) for piece in got]


def block_order():
    n = lax.axis_size("chip")
    return (lax.axis_index("chip") - jnp.arange(n)) % n


def core_order():
    return (lax.axis_index("core") + jnp.arange(2)) % 2


def match_order(wk):
    n = lax.axis_size("chip")
    taps, in_chan, cols = wk.shape
    blocks = jnp.take(wk.reshape(taps, n, 2, in_chan // (2 * n), cols), block_order(), axis=1)
    blocks = jnp.take(blocks, core_order(), axis=2)
    return blocks.transpose(0, 2, 1, 3, 4).reshape(taps, in_chan, cols)


def body(volume, w_first, b_first, w_second, b_second):
    chan_local, slab_depth, cell_count = volume.shape
    taps, in_local, out_chan = w_first.shape
    peers = lax.axis_size(CHAN)
    out_local = out_chan // peers
    sent = per_destination(w_first, peers)
    got = lax.all_to_all(sent, CHAN, 0, 0, tiled=True)
    n = lax.axis_size("chip")
    got = jnp.take(got.reshape((n, peers // n) + got.shape[1:]), block_order(), axis=0)
    got = jnp.take(got, core_order(), axis=1)
    w1k = got.transpose(2, 1, 0, 3, 4).reshape(3, peers * in_local, 9 * out_local)
    first_sum, w_second = layer(
        w1k, [gather_chan(volume[:, p]) for p in range(slab_depth)], w_second
    )
    w2k = match_order(kernel_filters(w_second))
    hidden = jnp.maximum(first_sum + b_first[None, :, None], 0.0).astype(jnp.bfloat16)
    second_sum, _ = layer(w2k, [gather_chan(hidden[p]) for p in range(slab_depth)])
    block_out = (second_sum + b_second[None, :, None]).astype(jnp.bfloat16)
    return block_out.transpose(1, 0, 2)


def solution(mesh):
    depth, chan = mesh.devices.shape
    split = jax.sharding.Mesh(mesh.devices.reshape(depth, chan // 2, 2), ("depth",) + CHAN)
    in_specs = (
        P(CHAN, "depth", None),
        P(None, CHAN, None),
        P(CHAN),
        P(None, None, CHAN),
        P(CHAN),
    )
    out_specs = P(CHAN, "depth", None)
    return jax.shard_map(body, mesh=split, in_specs=in_specs, out_specs=out_specs, check_vma=False)
```

```python
import functools

import jax
import jax.numpy as jnp
from jax import lax
from jax.experimental import pallas as pl
from jax.experimental.pallas import tpu as pltpu
from jax.sharding import PartitionSpec as P

W = 64


def plane_kernel(taps, w_ref, *refs):
    x_refs, out_refs = refs[: -len(taps)], refs[-len(taps) :]
    out_chan = out_refs[0].shape[0]
    cell_count = x_refs[0].shape[1]
    x = jnp.concatenate([r[...] for r in x_refs], 0)
    cell = lax.broadcasted_iota(jnp.int32, (out_chan, cell_count), 1)
    row = lax.shift_right_logical(cell, W.bit_length() - 1)
    col = cell & (W - 1)
    rows = cell_count // W
    masks = []
    for kh in range(3):
        for kw in range(3):
            ok = None
            if kh == 0:
                ok = row >= 1
            elif kh == 2:
                ok = row < rows - 1
            if kw == 0:
                ok = (col >= 1) if ok is None else ok & (col >= 1)
            elif kw == 2:
                ok = (col < W - 1) if ok is None else ok & (col < W - 1)
            masks.append(ok)
    for out_ref, kd in zip(out_refs, taps):
        z = lax.dot_general(
            w_ref[kd], x, (((0,), (0,)), ((), ())), preferred_element_type=jnp.float32
        )
        acc = None
        for kh in range(3):
            for kw in range(3):
                t = kh * 3 + kw
                shift = (kh - 1) * W + (kw - 1)
                zt = z[t * out_chan : (t + 1) * out_chan]
                if shift != 0:
                    zt = pltpu.roll(zt, (-shift) % cell_count, 1)
                if masks[t] is not None:
                    zt = jnp.where(masks[t], zt, 0.0)
                acc = zt if acc is None else acc + zt
        out_ref[...] = acc


def prep_kernel(w_ref, o_ref):
    dests, _, c_in, lanes = o_ref.shape
    out_local = w_ref.shape[2] // dests
    width = max(lanes, w_ref.shape[2])
    lane = lax.broadcasted_iota(jnp.int32, (c_in, width), 1)
    pad = width - w_ref.shape[2]
    for kd in range(3):
        rows = [w_ref[kd * 9 + t].astype(jnp.float32) for t in range(9)]
        if pad:
            rows = [jnp.concatenate([r, jnp.zeros((c_in, pad), r.dtype)], 1) for r in rows]
        for dest in range(dests):
            acc = jnp.zeros((c_in, width), jnp.float32)
            for t in range(9):
                shift = (t - dest) * out_local % width
                moved = pltpu.roll(rows[t], shift, 1) if shift else rows[t]
                ok = (lane >= t * out_local) & (lane < (t + 1) * out_local)
                acc = jnp.where(ok, moved, acc)
            o_ref[dest, kd] = acc[:, :lanes].astype(o_ref.dtype)


def per_destination(w_first, dests):
    taps, c_in, out_chan = w_first.shape
    lanes = 9 * (out_chan // dests)
    return pl.pallas_call(
        prep_kernel,
        out_shape=jax.ShapeDtypeStruct((dests, 3, c_in, lanes), w_first.dtype),
    )(w_first)


def plane_partials(wk, pieces, taps):
    out_chan = wk.shape[2] // 9
    cell_count = pieces[0].shape[1]
    return pl.pallas_call(
        functools.partial(plane_kernel, taps),
        out_shape=[jax.ShapeDtypeStruct((out_chan, cell_count), jnp.float32)] * len(taps),
        compiler_params=pltpu.CompilerParams(vmem_limit_bytes=48 * 1024 * 1024),
    )(wk, *pieces)


def kernel_filters(filters):
    taps, in_chan, out_chan = filters.shape
    f = filters.reshape(3, 9, in_chan, out_chan).transpose(0, 2, 1, 3)
    return f.reshape(3, in_chan, 9 * out_chan)


def layer(wk, planes, carry=None):
    outer = [plane_partials(wk, plane, (0, 2)) for plane in planes]
    outer, carry = lax.optimization_barrier((outer, carry))
    peers = lax.axis_size("depth")
    up = [(i, i + 1) for i in range(peers - 1)]
    down = [(j, i) for i, j in up]
    from_below = lax.ppermute(outer[-1][0], "depth", up)
    from_above = lax.ppermute(outer[0][1], "depth", down)
    count = len(planes)
    lower = [from_below] + [outer[p - 1][0] for p in range(1, count)]
    upper = [outer[p + 1][1] for p in range(count - 1)] + [from_above]
    middle = [plane_partials(wk, plane, (1,))[0] for plane in planes]
    return jnp.stack([middle[p] + lower[p] + upper[p] for p in range(count)], 0), carry


CHAN = ("chip", "core")


def gather_chan(local):
    n = lax.axis_size("chip")
    got = [local] + [
        lax.ppermute(local, "chip", [(i, (i + k) % n) for i in range(n)]) for k in range(1, n)
    ]
    swap = [(0, 1), (1, 0)]
    return got + [lax.ppermute(piece, "core", swap) for piece in got]


def block_order():
    n = lax.axis_size("chip")
    return (lax.axis_index("chip") - jnp.arange(n)) % n


def core_order():
    return (lax.axis_index("core") + jnp.arange(2)) % 2


def match_order(wk):
    n = lax.axis_size("chip")
    taps, in_chan, cols = wk.shape
    blocks = jnp.take(wk.reshape(taps, n, 2, in_chan // (2 * n), cols), block_order(), axis=1)
    blocks = jnp.take(blocks, core_order(), axis=2)
    return blocks.transpose(0, 2, 1, 3, 4).reshape(taps, in_chan, cols)


def body(volume, w_first, b_first, w_second, b_second):
    chan_local, slab_depth, cell_count = volume.shape
    taps, in_local, out_chan = w_first.shape
    peers = lax.axis_size(CHAN)
    out_local = out_chan // peers
    sent = per_destination(w_first, peers)
    got = lax.all_to_all(sent, CHAN, 0, 0, tiled=True)
    n = lax.axis_size("chip")
    got = jnp.take(got.reshape((n, peers // n) + got.shape[1:]), block_order(), axis=0)
    got = jnp.take(got, core_order(), axis=1)
    w1k = got.transpose(2, 1, 0, 3, 4).reshape(3, peers * in_local, 9 * out_local)
    first_sum, w_second = layer(
        w1k, [gather_chan(volume[:, p]) for p in range(slab_depth)], w_second
    )
    w2k = match_order(kernel_filters(w_second))
    hidden = jnp.maximum(first_sum + b_first[None, :, None], 0.0).astype(jnp.bfloat16)
    second_sum, _ = layer(w2k, [gather_chan(hidden[p]) for p in range(slab_depth)])
    block_out = (second_sum + b_second[None, :, None]).astype(jnp.bfloat16)
    return block_out.transpose(1, 0, 2)


def solution(mesh):
    depth, chan = mesh.devices.shape
    split = jax.sharding.Mesh(mesh.devices.reshape(depth, chan // 2, 2), ("depth",) + CHAN)
    in_specs = (
        P(CHAN, "depth", None),
        P(None, CHAN, None),
        P(CHAN),
        P(None, None, CHAN),
        P(CHAN),
    )
    out_specs = P(CHAN, "depth", None)
    return jax.shard_map(body, mesh=split, in_specs=in_specs, out_specs=out_specs, check_vma=False)
```

```python
import functools

import jax
import jax.numpy as jnp
from jax import lax
from jax.experimental import pallas as pl
from jax.experimental.pallas import tpu as pltpu
from jax.sharding import PartitionSpec as P

W = 64


def plane_kernel(taps, w_ref, *refs):
    x_refs, out_refs = refs[: -len(taps)], refs[-len(taps) :]
    out_chan = out_refs[0].shape[0]
    cell_count = x_refs[0].shape[1]
    x = jnp.concatenate([r[...] for r in x_refs], 0)
    cell = lax.broadcasted_iota(jnp.int32, (out_chan, cell_count), 1)
    row = lax.shift_right_logical(cell, W.bit_length() - 1)
    col = cell & (W - 1)
    rows = cell_count // W
    masks = []
    for kh in range(3):
        for kw in range(3):
            ok = None
            if kh == 0:
                ok = row >= 1
            elif kh == 2:
                ok = row < rows - 1
            if kw == 0:
                ok = (col >= 1) if ok is None else ok & (col >= 1)
            elif kw == 2:
                ok = (col < W - 1) if ok is None else ok & (col < W - 1)
            masks.append(ok)
    for out_ref, kd in zip(out_refs, taps):
        z = lax.dot_general(
            w_ref[kd], x, (((0,), (0,)), ((), ())), preferred_element_type=jnp.float32
        )
        acc = None
        for kh in range(3):
            for kw in range(3):
                t = kh * 3 + kw
                shift = (kh - 1) * W + (kw - 1)
                zt = z[t * out_chan : (t + 1) * out_chan]
                if shift != 0:
                    zt = pltpu.roll(zt, (-shift) % cell_count, 1)
                if masks[t] is not None:
                    zt = jnp.where(masks[t], zt, 0.0)
                acc = zt if acc is None else acc + zt
        out_ref[...] = acc


def prep_kernel(w_ref, o_ref):
    dests, _, c_in, lanes = o_ref.shape
    out_local = w_ref.shape[2] // dests
    width = max(lanes, w_ref.shape[2])
    lane = lax.broadcasted_iota(jnp.int32, (c_in, width), 1)
    pad = width - w_ref.shape[2]
    for kd in range(3):
        rows = [w_ref[kd * 9 + t].astype(jnp.float32) for t in range(9)]
        if pad:
            rows = [jnp.concatenate([r, jnp.zeros((c_in, pad), r.dtype)], 1) for r in rows]
        for dest in range(dests):
            acc = jnp.zeros((c_in, width), jnp.float32)
            for t in range(9):
                shift = (t - dest) * out_local % width
                moved = pltpu.roll(rows[t], shift, 1) if shift else rows[t]
                ok = (lane >= t * out_local) & (lane < (t + 1) * out_local)
                acc = jnp.where(ok, moved, acc)
            o_ref[dest, kd] = acc[:, :lanes].astype(o_ref.dtype)


def per_destination(w_first, dests):
    taps, c_in, out_chan = w_first.shape
    lanes = 9 * (out_chan // dests)
    return pl.pallas_call(
        prep_kernel,
        out_shape=jax.ShapeDtypeStruct((dests, 3, c_in, lanes), w_first.dtype),
    )(w_first)


def plane_partials(wk, pieces, taps):
    out_chan = wk.shape[2] // 9
    cell_count = pieces[0].shape[1]
    return pl.pallas_call(
        functools.partial(plane_kernel, taps),
        out_shape=[jax.ShapeDtypeStruct((out_chan, cell_count), jnp.float32)] * len(taps),
        compiler_params=pltpu.CompilerParams(vmem_limit_bytes=48 * 1024 * 1024),
    )(wk, *pieces)


def kernel_filters(filters):
    taps, in_chan, out_chan = filters.shape
    f = filters.reshape(3, 9, in_chan, out_chan).transpose(0, 2, 1, 3)
    return f.reshape(3, in_chan, 9 * out_chan)


def layer(wk, planes, carry=None):
    outer = [plane_partials(wk, plane, (0, 2)) for plane in planes]
    outer, carry = lax.optimization_barrier((outer, carry))
    peers = lax.axis_size("depth")
    up = [(i, i + 1) for i in range(peers - 1)]
    down = [(j, i) for i, j in up]
    from_below = lax.ppermute(outer[-1][0], "depth", up)
    from_above = lax.ppermute(outer[0][1], "depth", down)
    count = len(planes)
    lower = [from_below] + [outer[p - 1][0] for p in range(1, count)]
    upper = [outer[p + 1][1] for p in range(count - 1)] + [from_above]
    middle = [plane_partials(wk, plane, (1,))[0] for plane in planes]
    return jnp.stack([middle[p] + lower[p] + upper[p] for p in range(count)], 0), carry


CHAN = ("chip", "core")


def gather_chan(local):
    n = lax.axis_size("chip")
    far_first = sorted(range(1, n), key=lambda k: -min(k, n - k))
    sent = {k: lax.ppermute(local, "chip", [(i, (i + k) % n) for i in range(n)]) for k in far_first}
    got = [local] + [sent[k] for k in range(1, n)]
    swap = [(0, 1), (1, 0)]
    return got + [lax.ppermute(piece, "core", swap) for piece in got]


def block_order():
    n = lax.axis_size("chip")
    return (lax.axis_index("chip") - jnp.arange(n)) % n


def core_order():
    return (lax.axis_index("core") + jnp.arange(2)) % 2


def match_order(wk):
    n = lax.axis_size("chip")
    taps, in_chan, cols = wk.shape
    blocks = jnp.take(wk.reshape(taps, n, 2, in_chan // (2 * n), cols), block_order(), axis=1)
    blocks = jnp.take(blocks, core_order(), axis=2)
    return blocks.transpose(0, 2, 1, 3, 4).reshape(taps, in_chan, cols)


def body(volume, w_first, b_first, w_second, b_second):
    chan_local, slab_depth, cell_count = volume.shape
    taps, in_local, out_chan = w_first.shape
    peers = lax.axis_size(CHAN)
    out_local = out_chan // peers
    sent = per_destination(w_first, peers)
    got = lax.all_to_all(sent, CHAN, 0, 0, tiled=True)
    n = lax.axis_size("chip")
    got = jnp.take(got.reshape((n, peers // n) + got.shape[1:]), block_order(), axis=0)
    got = jnp.take(got, core_order(), axis=1)
    w1k = got.transpose(2, 1, 0, 3, 4).reshape(3, peers * in_local, 9 * out_local)
    first_sum, w_second = layer(
        w1k, [gather_chan(volume[:, p]) for p in range(slab_depth)], w_second
    )
    w2k = match_order(kernel_filters(w_second))
    hidden = jnp.maximum(first_sum + b_first[None, :, None], 0.0).astype(jnp.bfloat16)
    second_sum, _ = layer(w2k, [gather_chan(hidden[p]) for p in range(slab_depth)])
    block_out = (second_sum + b_second[None, :, None]).astype(jnp.bfloat16)
    return block_out.transpose(1, 0, 2)


def solution(mesh):
    depth, chan = mesh.devices.shape
    split = jax.sharding.Mesh(mesh.devices.reshape(depth, chan // 2, 2), ("depth",) + CHAN)
    in_specs = (
        P(CHAN, "depth", None),
        P(None, CHAN, None),
        P(CHAN),
        P(None, None, CHAN),
        P(CHAN),
    )
    out_specs = P(CHAN, "depth", None)
    return jax.shard_map(body, mesh=split, in_specs=in_specs, out_specs=out_specs, check_vma=False)
```

```python
import functools

import jax
import jax.numpy as jnp
from jax import lax
from jax.experimental import pallas as pl
from jax.experimental.pallas import tpu as pltpu
from jax.sharding import PartitionSpec as P

W = 64


def plane_kernel(taps, w_ref, *refs):
    x_refs, out_refs = refs[: -len(taps)], refs[-len(taps) :]
    out_chan = out_refs[0].shape[0]
    cell_count = x_refs[0].shape[1]
    x = jnp.concatenate([r[...] for r in x_refs], 0)
    cell = lax.broadcasted_iota(jnp.int32, (out_chan, cell_count), 1)
    row = lax.shift_right_logical(cell, W.bit_length() - 1)
    col = cell & (W - 1)
    rows = cell_count // W
    masks = []
    for kh in range(3):
        for kw in range(3):
            ok = None
            if kh == 0:
                ok = row >= 1
            elif kh == 2:
                ok = row < rows - 1
            if kw == 0:
                ok = (col >= 1) if ok is None else ok & (col >= 1)
            elif kw == 2:
                ok = (col < W - 1) if ok is None else ok & (col < W - 1)
            masks.append(ok)
    for out_ref, kd in zip(out_refs, taps):
        z = lax.dot_general(
            w_ref[kd], x, (((0,), (0,)), ((), ())), preferred_element_type=jnp.float32
        )
        acc = None
        for kh in range(3):
            for kw in range(3):
                t = kh * 3 + kw
                shift = (kh - 1) * W + (kw - 1)
                zt = z[t * out_chan : (t + 1) * out_chan]
                if shift != 0:
                    zt = pltpu.roll(zt, (-shift) % cell_count, 1)
                if masks[t] is not None:
                    zt = jnp.where(masks[t], zt, 0.0)
                acc = zt if acc is None else acc + zt
        out_ref[...] = acc


def prep_kernel(w_ref, o_ref):
    dests, _, c_in, lanes = o_ref.shape
    out_local = w_ref.shape[2] // dests
    width = max(lanes, w_ref.shape[2])
    lane = lax.broadcasted_iota(jnp.int32, (c_in, width), 1)
    pad = width - w_ref.shape[2]
    for kd in range(3):
        rows = [w_ref[kd * 9 + t].astype(jnp.float32) for t in range(9)]
        if pad:
            rows = [jnp.concatenate([r, jnp.zeros((c_in, pad), r.dtype)], 1) for r in rows]
        for dest in range(dests):
            acc = jnp.zeros((c_in, width), jnp.float32)
            for t in range(9):
                shift = (t - dest) * out_local % width
                moved = pltpu.roll(rows[t], shift, 1) if shift else rows[t]
                ok = (lane >= t * out_local) & (lane < (t + 1) * out_local)
                acc = jnp.where(ok, moved, acc)
            o_ref[dest, kd] = acc[:, :lanes].astype(o_ref.dtype)


def per_destination(w_first, dests):
    taps, c_in, out_chan = w_first.shape
    lanes = 9 * (out_chan // dests)
    return pl.pallas_call(
        prep_kernel,
        out_shape=jax.ShapeDtypeStruct((dests, 3, c_in, lanes), w_first.dtype),
    )(w_first)


def plane_partials(wk, pieces, taps):
    out_chan = wk.shape[2] // 9
    cell_count = pieces[0].shape[1]
    return pl.pallas_call(
        functools.partial(plane_kernel, taps),
        out_shape=[jax.ShapeDtypeStruct((out_chan, cell_count), jnp.float32)] * len(taps),
        compiler_params=pltpu.CompilerParams(vmem_limit_bytes=48 * 1024 * 1024),
    )(wk, *pieces)


def kernel_filters(filters):
    taps, in_chan, out_chan = filters.shape
    f = filters.reshape(3, 9, in_chan, out_chan).transpose(0, 2, 1, 3)
    return f.reshape(3, in_chan, 9 * out_chan)


def layer(wk, planes, carry=None):
    outer = [plane_partials(wk, plane, (0, 2)) for plane in planes]
    outer, carry = lax.optimization_barrier((outer, carry))
    peers = lax.axis_size("depth")
    up = [(i, i + 1) for i in range(peers - 1)]
    down = [(j, i) for i, j in up]
    from_below = lax.ppermute(outer[-1][0], "depth", up)
    from_above = lax.ppermute(outer[0][1], "depth", down)
    count = len(planes)
    lower = [from_below] + [outer[p - 1][0] for p in range(1, count)]
    upper = [outer[p + 1][1] for p in range(count - 1)] + [from_above]
    middle = [plane_partials(wk, plane, (1,))[0] for plane in planes]
    return jnp.stack([middle[p] + lower[p] + upper[p] for p in range(count)], 0), carry


CHAN = ("chip", "core")


def gather_chan(local):
    n = lax.axis_size("chip")
    got = [local] + [
        lax.ppermute(local, "chip", [(i, (i + k) % n) for i in range(n)]) for k in range(1, n)
    ]
    swap = [(0, 1), (1, 0)]
    return got + [lax.ppermute(piece, "core", swap) for piece in got]


def block_order():
    n = lax.axis_size("chip")
    return (lax.axis_index("chip") - jnp.arange(n)) % n


def core_order():
    return (lax.axis_index("core") + jnp.arange(2)) % 2


def match_order(wk):
    n = lax.axis_size("chip")
    taps, in_chan, cols = wk.shape
    blocks = jnp.take(wk.reshape(taps, n, 2, in_chan // (2 * n), cols), block_order(), axis=1)
    blocks = jnp.take(blocks, core_order(), axis=2)
    return blocks.transpose(0, 2, 1, 3, 4).reshape(taps, in_chan, cols)


def body(volume, w_first, b_first, w_second, b_second):
    chan_local, slab_depth, cell_count = volume.shape
    taps, in_local, out_chan = w_first.shape
    peers = lax.axis_size(CHAN)
    out_local = out_chan // peers
    sent = per_destination(w_first, peers)
    n = lax.axis_size("chip")
    across = lax.all_to_all(sent.reshape((n, peers // n) + sent.shape[1:]), "chip", 0, 0, tiled=True)
    across = jnp.take(across, core_order(), axis=1)
    other = lax.ppermute(across[:, 1], "core", [(0, 1), (1, 0)])
    got = jnp.stack([across[:, 0], other], 0)
    got = jnp.take(got, block_order(), axis=1)
    w1k = got.transpose(2, 0, 1, 3, 4).reshape(3, peers * in_local, 9 * out_local)
    first_sum, w_second = layer(
        w1k, [gather_chan(volume[:, p]) for p in range(slab_depth)], w_second
    )
    w2k = match_order(kernel_filters(w_second))
    hidden = jnp.maximum(first_sum + b_first[None, :, None], 0.0).astype(jnp.bfloat16)
    second_sum, _ = layer(w2k, [gather_chan(hidden[p]) for p in range(slab_depth)])
    block_out = (second_sum + b_second[None, :, None]).astype(jnp.bfloat16)
    return block_out.transpose(1, 0, 2)


def solution(mesh):
    depth, chan = mesh.devices.shape
    split = jax.sharding.Mesh(mesh.devices.reshape(depth, chan // 2, 2), ("depth",) + CHAN)
    in_specs = (
        P(CHAN, "depth", None),
        P(None, CHAN, None),
        P(CHAN),
        P(None, None, CHAN),
        P(CHAN),
    )
    out_specs = P(CHAN, "depth", None)
    return jax.shard_map(body, mesh=split, in_specs=in_specs, out_specs=out_specs, check_vma=False)
```

```python
import functools

import jax
import jax.numpy as jnp
from jax import lax
from jax.experimental import pallas as pl
from jax.experimental.pallas import tpu as pltpu
from jax.sharding import PartitionSpec as P


W = 64


def plane_kernel(taps, w_ref, *refs):
    x_refs, out_refs = refs[: -len(taps)], refs[-len(taps) :]
    out_chan = out_refs[0].shape[0]
    cell_count = x_refs[0].shape[1]
    x = jnp.concatenate([r[...] for r in x_refs], 0)
    cell = lax.broadcasted_iota(jnp.int32, (out_chan, cell_count), 1)
    row = lax.shift_right_logical(cell, W.bit_length() - 1)
    col = cell & (W - 1)
    rows = cell_count // W
    masks = []
    for kh in range(3):
        for kw in range(3):
            ok = None
            if kh == 0:
                ok = row >= 1
            elif kh == 2:
                ok = row < rows - 1
            if kw == 0:
                ok = (col >= 1) if ok is None else ok & (col >= 1)
            elif kw == 2:
                ok = (col < W - 1) if ok is None else ok & (col < W - 1)
            masks.append(ok)
    for out_ref, kd in zip(out_refs, taps):
        z = lax.dot_general(
            w_ref[kd], x, (((0,), (0,)), ((), ())), preferred_element_type=jnp.float32
        )
        acc = None
        for kh in range(3):
            for kw in range(3):
                t = kh * 3 + kw
                shift = (kh - 1) * W + (kw - 1)
                zt = z[t * out_chan : (t + 1) * out_chan]
                if shift != 0:
                    zt = pltpu.roll(zt, (-shift) % cell_count, 1)
                if masks[t] is not None:
                    zt = jnp.where(masks[t], zt, 0.0)
                acc = zt if acc is None else acc + zt
        out_ref[...] = acc


def prep_kernel(w_ref, o_ref):
    dests, _, c_in, lanes = o_ref.shape
    out_local = w_ref.shape[2] // dests
    width = max(lanes, w_ref.shape[2])
    lane = lax.broadcasted_iota(jnp.int32, (c_in, width), 1)
    pad = width - w_ref.shape[2]
    for kd in range(3):
        rows = [w_ref[kd * 9 + t].astype(jnp.float32) for t in range(9)]
        if pad:
            rows = [jnp.concatenate([r, jnp.zeros((c_in, pad), r.dtype)], 1) for r in rows]
        for dest in range(dests):
            acc = jnp.zeros((c_in, width), jnp.float32)
            for t in range(9):
                shift = (t - dest) * out_local % width
                moved = pltpu.roll(rows[t], shift, 1) if shift else rows[t]
                ok = (lane >= t * out_local) & (lane < (t + 1) * out_local)
                acc = jnp.where(ok, moved, acc)
            o_ref[dest, kd] = acc[:, :lanes].astype(o_ref.dtype)


def per_destination(w_first, dests):
    _, c_in, out_chan = w_first.shape
    lanes = 9 * (out_chan // dests)
    return pl.pallas_call(
        prep_kernel,
        out_shape=jax.ShapeDtypeStruct((dests, 3, c_in, lanes), w_first.dtype),
    )(w_first)


def plane_partials(wk, pieces, taps):
    out_chan = wk.shape[2] // 9
    cell_count = pieces[0].shape[1]
    return pl.pallas_call(
        functools.partial(plane_kernel, taps),
        out_shape=[jax.ShapeDtypeStruct((out_chan, cell_count), jnp.float32)] * len(taps),
        compiler_params=pltpu.CompilerParams(vmem_limit_bytes=48 * 1024 * 1024),
    )(wk, *pieces)


def kernel_filters(filters):
    _, in_chan, out_chan = filters.shape
    f = filters.reshape(3, 9, in_chan, out_chan).transpose(0, 2, 1, 3)
    return f.reshape(3, in_chan, 9 * out_chan)


def layer(wk, planes, carry=None):
    outer = [plane_partials(wk, plane, (0, 2)) for plane in planes]
    outer, carry = lax.optimization_barrier((outer, carry))
    peers = lax.axis_size("depth")
    up = [(i, i + 1) for i in range(peers - 1)]
    down = [(j, i) for i, j in up]
    from_below = lax.ppermute(outer[-1][0], "depth", up)
    from_above = lax.ppermute(outer[0][1], "depth", down)
    count = len(planes)
    lower = [from_below] + [outer[p - 1][0] for p in range(1, count)]
    upper = [outer[p + 1][1] for p in range(count - 1)] + [from_above]
    middle = [plane_partials(wk, plane, (1,))[0] for plane in planes]
    return jnp.stack([middle[p] + lower[p] + upper[p] for p in range(count)], 0), carry


CHAN = ("chip", "core")


def gather_chan(local):
    n = lax.axis_size("chip")
    got = [local]
    for k in range(1, n):
        got.append(lax.ppermute(local, "chip", [(i, (i + k) % n) for i in range(n)]))
    swap = [(0, 1), (1, 0)]
    return got + [lax.ppermute(piece, "core", swap) for piece in got]


def block_order():
    n = lax.axis_size("chip")
    return (lax.axis_index("chip") - jnp.arange(n)) % n


def core_order():
    return (lax.axis_index("core") + jnp.arange(2)) % 2


def match_order(wk):
    n = lax.axis_size("chip")
    taps, in_chan, cols = wk.shape
    blocks = jnp.take(wk.reshape(taps, n, 2, in_chan // (2 * n), cols), block_order(), axis=1)
    blocks = jnp.take(blocks, core_order(), axis=2)
    return blocks.transpose(0, 2, 1, 3, 4).reshape(taps, in_chan, cols)


def block(volume, w_first, b_first, w_second, b_second):
    _, slab_depth, _ = volume.shape
    _, in_local, out_chan = w_first.shape
    peers = lax.axis_size(CHAN)
    out_local = out_chan // peers
    sent = per_destination(w_first, peers)
    got = lax.all_to_all(sent, CHAN, 0, 0, tiled=True)
    n = lax.axis_size("chip")
    got = jnp.take(got.reshape((n, peers // n) + got.shape[1:]), block_order(), axis=0)
    got = jnp.take(got, core_order(), axis=1)
    w1k = got.transpose(2, 1, 0, 3, 4).reshape(3, peers * in_local, 9 * out_local)
    first_sum, w_second = layer(
        w1k, [gather_chan(volume[:, p]) for p in range(slab_depth)], w_second
    )
    w2k = match_order(kernel_filters(w_second))
    hidden = jnp.maximum(first_sum + b_first[None, :, None], 0.0).astype(jnp.bfloat16)
    second_sum, _ = layer(w2k, [gather_chan(hidden[p]) for p in range(slab_depth)])
    block_out = (second_sum + b_second[None, :, None]).astype(jnp.bfloat16)
    return block_out.transpose(1, 0, 2)


def solution(mesh):
    depth, chan = mesh.devices.shape
    split = jax.sharding.Mesh(mesh.devices.reshape(depth, chan // 2, 2), ("depth",) + CHAN)
    in_specs = (
        P(CHAN, "depth", None),
        P(None, CHAN, None),
        P(CHAN),
        P(None, None, CHAN),
        P(CHAN),
    )
    out_specs = P(CHAN, "depth", None)
    return jax.shard_map(block, mesh=split, in_specs=in_specs, out_specs=out_specs, check_vma=False)
```
